256 devices in a mesh: tok: 32 (over x, z), head: 8 (over y, core).
Axes of the slice: x: 4, y: 4, z: 8, core: 2. Of those that a mesh axis runs over, the one named last changes fastest.
Arguments:
- tokens: bfloat16 [32768, 1664], P(('tok', 'head')), may hold values from -75 to 75
- attn_gain: float32 [1664], replicated, may hold values from 0.1 to 1.9
- qkv_weight: bfloat16 [3, 1664, 1664], P(None, 'head'), may hold values from -5 to 5
- out_weight: bfloat16 [1664, 1664], P('head'), may hold values from -0.4375 to 0.4375
- merge_gain: float32 [1664], replicated, may hold values from 0.1 to 1.9
- merge_weight: bfloat16 [6656, 4096], P('head', 'tok'), may hold values from -0.078125 to 0.078125
- grid_sizes: int32 [2, 128], P(None, 'tok'), may hold values from 2 to 16, as said below
- segment_ids: int32 [32768], P('tok'), may hold values from 0 to 127, as said below
- patch_pos: int32 [2, 32768], P(None, 'tok'), may hold values from 0 to 15, as said below
- live_mask: int32 [32768], P('tok'), may hold values from 0 to 1, as said below
- owners: int32 [8192, 1], P(('tok', 'head')), may hold values from 0 to 31; in each aligned block of 32 rows (0 to 31, 32 to 63, ...) at most 2 rows name the same one
Outputs:
- delivered: bfloat16 [16384, 4096], P(('tok', 'head'))
The draws below stay inside these ranges and needn't reach their ends.
Inputs may be any that keep to these rules, and one draw needn't show every extreme that they name: `grid_sizes`: both sides of every image are even, and some image is 16 by 16. `segment_ids`: never fall along the tokens. The aligned block b of 1024 tokens holds images b * 4 to (b + 1) * 4 - 1 packed in order from the block's start, image s taking grid_sizes[0, s] * grid_sizes[1, s] tokens; the block's remaining tokens carry the number of its last image. `patch_pos`: an image's tokens come in 2x2 windows, windows in row-major order, each window as (2 * r, 2 * c), (2 * r, 2 * c + 1), (2 * r + 1, 2 * c), (2 * r + 1, 2 * c + 1); padding tokens sit at (0, 0). `live_mask`: 1 exactly on the tokens that belong to an image. `owners`: in each aligned block of 32 rows (the merged rows of one device) no owner is named more than 2 times.
All inputs are finite; a program needn't handle non-finite values.
Results may differ from the reference program's by a relative error of at most 0.024.
Values may be sent and summed in bfloat16 or wider, within the bound.
No kernel may reach another device: no remote copies, remote signals or barrier semaphores. Data moves between devices by JAX's collectives and lax.ppermute only.
A program may use at most 64 MiB of HBM per device.

```python
import math
import jax
import jax.numpy as jnp
import numpy as np
from jax import lax

D = 1664
HEADS = 16
HD = 104
OUT = 4096
SIDE = 16
GROUP = 1024
TOKENS = 32768
IMG_GRP = 4
MDEV = 32
MERGED = 8192
CAP = 2
SLOTS = 64
N_TOK = 32
N_HEAD = 8


def packing(key):
    base_key = jax.random.fold_in(key, 31)
    half_side = SIDE // 2
    half_low = max(1, 3 * SIDE // 8)
    heights = 2 * jax.random.randint(jax.random.fold_in(base_key, 1), (N_TOK, IMG_GRP), half_low, half_side + 1, dtype=jnp.int32)
    widths = 2 * jax.random.randint(jax.random.fold_in(base_key, 2), (N_TOK, IMG_GRP), half_low, half_side + 1, dtype=jnp.int32)
    heights = heights.at[0, 0].set(SIDE)
    widths = widths.at[0, 0].set(SIDE)
    image_area = heights * widths
    starts = jnp.cumsum(image_area, axis=1, dtype=jnp.int32) - image_area
    totals = jnp.sum(image_area, axis=1, dtype=jnp.int32)
    places = jnp.arange(GROUP, dtype=jnp.int32)
    started = (starts[:, None, :] <= places[None, :, None]).astype(jnp.int32)
    image_slot = jnp.sum(started, axis=2, dtype=jnp.int32) - 1
    slot_hot = (image_slot[:, :, None] == jnp.arange(IMG_GRP, dtype=jnp.int32)[None, None, :]).astype(jnp.int32)
    own_start = jnp.sum(slot_hot * starts[:, None, :], axis=2, dtype=jnp.int32)
    own_width = jnp.sum(slot_hot * widths[:, None, :], axis=2, dtype=jnp.int32)
    live_flag = (places[None, :] < totals[:, None]).astype(jnp.int32)
    offset = places[None, :] - own_start
    window = offset // 4
    within = offset % 4
    window_cols = own_width // 2
    row_pos = (2 * (window // window_cols) + within // 2) * live_flag
    col_pos = (2 * (window % window_cols) + within % 2) * live_flag
    segments = jnp.arange(N_TOK, dtype=jnp.int32)[:, None] * IMG_GRP + image_slot
    grid_table = jnp.stack([heights.reshape(-1), widths.reshape(-1)])
    positions = jnp.stack([row_pos.reshape(-1), col_pos.reshape(-1)])
    return (grid_table, segments.reshape(-1), positions, live_flag.reshape(-1))


def draw_grid_sizes(key, part):
    return packing(key)[0]


def draw_segment_ids(key, part):
    return packing(key)[1]


def draw_patch_pos(key, part):
    return packing(key)[2]


def draw_live_mask(key, part):
    return packing(key)[3]


def draw_tokens(key, part):
    key_noise, key_rows, key_cols = jax.random.split(key, 3)
    row_scale = jnp.exp(jax.random.uniform(key_rows, (TOKENS, 1), jnp.float32, math.log(0.5), math.log(5.0)))
    feature_ramp = 1.0 + 2.0 * jnp.arange(D, dtype=jnp.float32) / (D - 1)
    col_scale = jnp.exp(jax.random.uniform(key_cols, (1, D), jnp.float32, math.log(0.4), math.log(1.2))) * feature_ramp[None, :]
    base_noise = jnp.clip(jax.random.normal(key_noise, (TOKENS, D), jnp.float32), -4.0, 4.0)
    return (base_noise * row_scale * col_scale).astype(jnp.bfloat16)


def draw_qkv_weight(key, part):
    key_main = jax.random.fold_in(key, 0)
    weights = jnp.clip(jax.random.normal(key_main, (3, D, D), jnp.float32), -6.0, 6.0) / math.sqrt(D)
    return weights.astype(jnp.bfloat16)


def shard_levels(key, dims, shards, smallest, high):
    loudness, own = 1.0, jax.random.fold_in(key, 6)
    for position, shards_of in shards:
        steps = jnp.exp(jax.random.uniform(jax.random.fold_in(own, position), (shards_of,), jnp.float32, smallest / len(shards), high / len(shards)))
        loudness = loudness * jnp.repeat(steps, dims[position] // shards_of).reshape([-1 if axis == position else 1 for axis in range(len(dims))])
    return loudness


def routed_block(own_key, own, number, rows, amount, top, limit, slope):
    order = jax.random.permutation(own_key, amount)
    crowded, usual = load_shares(amount, rows * top, limit, slope, True), load_shares(amount, rows * top, limit, slope, False)
    places = jnp.arange(amount)

    def named(sizes, rotation):
        used = int((sizes > 0).sum())
        fixed = max(1, used // 4)
        moved = fixed + (places - fixed + rotation * (used - fixed)) % max(1, amount - fixed)
        return jnp.zeros((amount,), jnp.int32).at[order[jnp.where(places < fixed, places, moved)]].set(jnp.asarray(sizes, jnp.int32))

    sizes = jnp.where(number % 4 == 0, named(crowded, number // 4), named(usual, number - number // 4 - 1))
    mixed = jax.random.permutation(jax.random.fold_in(own, 3), amount)
    giver, receiver = mixed[0:amount // 2 * 2:2], mixed[1:amount // 2 * 2:2]
    room = jnp.minimum(sizes[giver] - 1, limit - sizes[receiver]) // 2
    room = jnp.where((giver == order[0]) | (receiver == order[0]) | (sizes[receiver] == 0), 0, jnp.maximum(room, 0))
    moved = jax.random.randint(jax.random.fold_in(own, 4), (amount // 2,), 0, 1 << 20) % (room + 1)
    sizes = sizes.at[giver].add(-moved).at[receiver].add(moved)
    labels = jnp.searchsorted(jnp.cumsum(sizes), jnp.arange(rows * top), side="right").astype(jnp.int32)
    grid = labels.reshape(top, rows).T
    grid = grid[jax.random.permutation(jax.random.fold_in(own, 1), rows)]
    rotation = jax.random.randint(jax.random.fold_in(own, 2), (rows, 1), 0, top)
    return jnp.take_along_axis(grid, (jnp.arange(top)[None, :] + rotation) % top, axis=1)


def load_shares(amount, total, most, slope, full):
    loads = [(1 << 20) // math.isqrt(grade ** slope) + 1 for grade in range(1, amount + 1)]
    largest = most if full else min(most, max(-(-total // amount), total * loads[0] // sum(loads)))
    least = 1 if total - largest >= amount - 1 else 0
    counts, rest = [largest] + [least] * (amount - 1), total - largest - least * (amount - 1)
    while rest > 0:
        movable = [i for i in range(1, amount) if counts[i] < largest] or [i for i in range(1, amount) if counts[i] < most]
        whole, remaining = sum([loads[i] for i in movable]), rest
        for i in movable:
            addition = min(most - counts[i], max(1, remaining * loads[i] // whole), rest)
            counts[i] = counts[i] + addition
            rest = rest - addition
    return np.array(counts)


def scatter_about(own_key, extent, width, limit, cuts=(), kind=jnp.bfloat16):
    result = width * jax.random.normal(own_key, extent, jnp.float32)
    if cuts:
        result = result * shard_levels(own_key, extent, cuts, -0.22, 0.18)
    return jnp.clip(result, -limit, limit).astype(kind)


def setup_inputs(seed: int = 0) -> dict:
    streams_of = jax.random.split(jax.random.key(seed), 12)
    tokens = draw_tokens(jax.random.fold_in(streams_of[11], 71), 0)
    attn_gain = jnp.clip(1.0 + 0.18 * jax.random.normal(streams_of[1], (D,), jnp.float32), 0.1, 1.9)
    qkv_weight = draw_qkv_weight(jax.random.fold_in(streams_of[11], 71), 0)
    out_weight = scatter_about(streams_of[3], (D, D), (2 * HD) ** -0.5, 0.4375, ((0, 8),))
    merge_gain = jnp.clip(1.0 + 0.18 * jax.random.normal(streams_of[4], (D,), jnp.float32), 0.1, 1.9)
    merge_weight = scatter_about(streams_of[5], (4 * D, OUT), (4 * D) ** -0.5, 0.078125, ((0, 8), (1, 32)))
    grid_sizes = draw_grid_sizes(jax.random.fold_in(streams_of[11], 71), 0)
    segment_ids = draw_segment_ids(jax.random.fold_in(streams_of[11], 71), 0)
    patch_pos = draw_patch_pos(jax.random.fold_in(streams_of[11], 71), 0)
    live_mask = draw_live_mask(jax.random.fold_in(streams_of[11], 71), 0)
    owners_keys = jax.random.split(jax.random.fold_in(streams_of[10], 1), MERGED // MDEV)
    owners_turns = jax.random.permutation(jax.random.fold_in(streams_of[10], 3), MERGED // MDEV)
    owners = jax.vmap(lambda own, number: routed_block(jax.random.fold_in(streams_of[10], 2), own, number, MDEV, N_TOK, 1, CAP, 2))(owners_keys, owners_turns).reshape((MERGED, 1))
    return dict(tokens=tokens, attn_gain=attn_gain, qkv_weight=qkv_weight, out_weight=out_weight, merge_gain=merge_gain, merge_weight=merge_weight, grid_sizes=grid_sizes, segment_ids=segment_ids, patch_pos=patch_pos, live_mask=live_mask, owners=owners)


EPSILON = 1e-06
NEGATIVE = -1e+30

def layer_norm(values, gain_vec):
    average = lax.optimization_barrier(jnp.mean(values, axis=-1, keepdims=True))
    centred = values - average
    variance = lax.optimization_barrier(jnp.mean(centred * centred, axis=-1, keepdims=True))
    return centred * lax.rsqrt(variance + EPSILON) * gain_vec

def rotate(vectors, row_coord, col_coord):
    quarter = vectors.shape[-1] // 4
    frequency = 10000.0 ** (-jnp.arange(quarter, dtype=jnp.float32) / quarter)
    pieces = []
    for which_axis, coordinate in ((0, row_coord), (1, col_coord)):
        leading = vectors[..., 2 * which_axis * quarter:(2 * which_axis + 1) * quarter]
        trailing = vectors[..., (2 * which_axis + 1) * quarter:(2 * which_axis + 2) * quarter]
        angles = coordinate[:, None, None] * frequency
        cosine = jnp.cos(angles)
        sine_val = jnp.sin(angles)
        pieces.append(leading * cosine - trailing * sine_val)
        pieces.append(leading * sine_val + trailing * cosine)
    return jnp.concatenate(pieces, axis=-1)

def attend(queries, key_rows, value_rows, segments, live_flag):
    positions = jnp.arange(segments.shape[0], dtype=jnp.int32)
    allowed = (segments[:, None] == segments[None, :]) & ((live_flag[None, :] == 1) | (positions[:, None] == positions[None, :]))

    def one_head(head_data):
        query_head, key_head, value_head = head_data
        scores = jnp.dot(query_head, key_head.T, preferred_element_type=jnp.float32)
        masked = jnp.where(allowed, scores, NEGATIVE)
        row_top = lax.optimization_barrier(jnp.max(masked, axis=1, keepdims=True))
        exponent = jnp.where(allowed, jnp.exp(masked - row_top), 0.0)
        denominator = lax.optimization_barrier(jnp.sum(exponent, axis=1, keepdims=True))
        numerator = jnp.dot(exponent.astype(jnp.bfloat16), value_head, preferred_element_type=jnp.float32)
        return (numerator / denominator).astype(jnp.bfloat16)
    stacked = (jnp.swapaxes(queries, 0, 1), jnp.swapaxes(key_rows, 0, 1), jnp.swapaxes(value_rows, 0, 1))
    return jnp.swapaxes(lax.map(one_head, stacked), 0, 1)

def reference(tokens, attn_gain, qkv_weight, out_weight, merge_gain, merge_weight, grid_sizes, segment_ids, patch_pos, live_mask, owners):
    picked = grid_sizes[:, segment_ids].astype(jnp.float32)
    coords = patch_pos.astype(jnp.float32) * SIDE / picked
    head_width = HEADS // N_HEAD * HD
    stacked_weight = qkv_weight.reshape(3 * D, D)

    def one_group(group_data):
        group_tokens, group_coords, group_segments, group_live = group_data
        normed = layer_norm(group_tokens.astype(jnp.float32), attn_gain).astype(jnp.bfloat16)
        projected_rows = lax.dot_general(normed, stacked_weight, (((1,), (1,)), ((), ())), preferred_element_type=jnp.float32).reshape(GROUP, 3, HEADS, HD)
        queries = (rotate(projected_rows[:, 0], group_coords[0], group_coords[1]) * HD ** (-0.5)).astype(jnp.bfloat16)
        key_rows = rotate(projected_rows[:, 1], group_coords[0], group_coords[1]).astype(jnp.bfloat16)
        value_rows = projected_rows[:, 2].astype(jnp.bfloat16)
        heads_out = attend(queries, key_rows, value_rows, group_segments, group_live).reshape(GROUP, D)
        attn_out = jnp.zeros((GROUP, D), jnp.float32)
        for member in range(N_HEAD):
            columns = heads_out[:, member * head_width:(member + 1) * head_width]
            head_term = jnp.dot(columns, out_weight[member * head_width:(member + 1) * head_width], preferred_element_type=jnp.float32)
            attn_out = attn_out + lax.optimization_barrier(head_term.astype(jnp.bfloat16)).astype(jnp.float32)
        stream = (group_tokens.astype(jnp.float32) + attn_out).reshape(GROUP // 4, 4, D)
        average = lax.optimization_barrier(jnp.mean(stream, axis=2, keepdims=True))
        variance = lax.optimization_barrier(jnp.mean(stream * stream, axis=2, keepdims=True)) - average * average
        normal_rows = (stream - average) * lax.rsqrt(variance + EPSILON) * merge_gain
        return normal_rows.astype(jnp.bfloat16).reshape(GROUP // 4, 4 * D)
    group_inputs = (tokens.reshape(N_TOK, GROUP, D), jnp.transpose(coords.reshape(2, N_TOK, GROUP), (1, 0, 2)), segment_ids.reshape(N_TOK, GROUP), live_mask.reshape(N_TOK, GROUP))
    merged = lax.map(one_group, group_inputs).reshape(MERGED, 4 * D)
    slice_width = 4 * D // N_HEAD
    summed = jnp.zeros((MERGED, OUT), jnp.float32)
    for member in range(N_HEAD):
        head_term = jnp.dot(merged[:, member * slice_width:(member + 1) * slice_width], merge_weight[member * slice_width:(member + 1) * slice_width], preferred_element_type=jnp.float32)
        summed = summed + lax.optimization_barrier(head_term.astype(jnp.bfloat16)).astype(jnp.float32)
    projected = summed.astype(jnp.bfloat16)
    block_rows = projected.reshape(N_TOK, N_HEAD, MDEV, OUT).astype(jnp.float32)
    owner_block = owners[:, 0].reshape(N_TOK, N_HEAD, MDEV)
    owner_hot = (owner_block[..., None] == jnp.arange(N_TOK, dtype=jnp.int32)).astype(jnp.int32)
    earlier = jnp.cumsum(owner_hot, axis=2, dtype=jnp.int32) - owner_hot
    slot_index = lax.optimization_barrier(jnp.sum(earlier * owner_hot, axis=3, dtype=jnp.int32))
    slot_hot = (slot_index[..., None] == jnp.arange(CAP, dtype=jnp.int32)).astype(jnp.float32)
    select = owner_hot.astype(jnp.float32)[..., None] * slot_hot[:, :, :, None, :]
    delivered = jnp.einsum('thmoc,thmf->ohtcf', select, block_rows, precision=lax.Precision.HIGHEST)
    return delivered.reshape(N_TOK * N_HEAD * SLOTS, OUT).astype(jnp.bfloat16)
```

```python
import jax
import jax.numpy as jnp
from jax import lax
from jax.sharding import PartitionSpec as P

D = 1664
HD = 104
SIDE = 16
CHUNKS = 2


EPSILON = 1e-06
NEGATIVE = -1e30


def layer_norm(values, gain_vec):
    average = jnp.mean(values, axis=-1, keepdims=True)
    centred = values - average
    variance = jnp.mean(centred * centred, axis=-1, keepdims=True)
    return centred * lax.rsqrt(variance + EPSILON) * gain_vec


def rotate(vectors, row_coord, col_coord):
    quarter = vectors.shape[-1] // 4
    frequency = 10000.0 ** (-jnp.arange(quarter, dtype=jnp.float32) / quarter)
    pieces = []
    for which_axis, coordinate in ((0, row_coord), (1, col_coord)):
        leading = vectors[..., 2 * which_axis * quarter : (2 * which_axis + 1) * quarter]
        trailing = vectors[..., (2 * which_axis + 1) * quarter : (2 * which_axis + 2) * quarter]
        angles = coordinate[:, None, None] * frequency
        cosine = jnp.cos(angles)
        sine_val = jnp.sin(angles)
        pieces.append(leading * cosine - trailing * sine_val)
        pieces.append(leading * sine_val + trailing * cosine)
    return jnp.concatenate(pieces, axis=-1)


def body(
    tokens,
    attn_gain,
    qkv_weight,
    out_weight,
    merge_gain,
    merge_weight,
    grid_sizes,
    segment_ids,
    patch_pos,
    live_mask,
    owners,
):
    group_len = segment_ids.shape[0]
    local_rows = tokens.shape[0]
    head_width = qkv_weight.shape[1]
    heads_here = head_width // HD
    tok_count = lax.axis_size("tok")
    image_count = grid_sizes.shape[1]
    local_image = segment_ids - lax.axis_index("tok") * image_count
    image_match = local_image[:, None] == jnp.arange(image_count, dtype=jnp.int32)[None, :]
    grid_float = grid_sizes.astype(jnp.float32)
    row_size = jnp.sum(jnp.where(image_match, grid_float[0][None, :], 0.0), axis=1)
    col_size = jnp.sum(jnp.where(image_match, grid_float[1][None, :], 0.0), axis=1)
    row_coord = patch_pos[0].astype(jnp.float32) * SIDE / row_size
    col_coord = patch_pos[1].astype(jnp.float32) * SIDE / col_size
    stacked_weight = qkv_weight.reshape(3 * head_width, D)
    normed = layer_norm(tokens.astype(jnp.float32), attn_gain).astype(jnp.bfloat16)
    projected_rows = lax.dot_general(
        lax.all_gather(normed, "head", axis=0, tiled=True),
        stacked_weight,
        (((1,), (1,)), ((), ())),
        preferred_element_type=jnp.float32,
    )
    projected_rows = projected_rows.reshape(group_len, 3, heads_here, HD)
    query_all = (rotate(projected_rows[:, 0], row_coord, col_coord) * HD ** (-0.5)).astype(
        jnp.bfloat16
    )
    key_all = rotate(projected_rows[:, 1], row_coord, col_coord).astype(jnp.bfloat16)
    value_all = projected_rows[:, 2].astype(jnp.bfloat16)
    block_len = min(512, group_len)
    block_count = group_len // block_len
    key_live = live_mask == 1

    def allowed_pairs(query_start, span):
        query_seg = lax.dynamic_slice_in_dim(segment_ids, query_start, block_len)
        query_place = query_start + jnp.arange(block_len, dtype=jnp.int32)
        key_place = jnp.arange(span, dtype=jnp.int32)
        same_image = query_seg[:, None] == segment_ids[None, :]
        return same_image & (key_live[None, :] | (query_place[:, None] == key_place[None, :]))

    def query_block(query_start):
        queries = lax.dynamic_slice_in_dim(query_all, query_start, block_len, 0)
        allowed = allowed_pairs(query_start, group_len)
        scores = jnp.einsum("qhd,khd->hqk", queries, key_all, preferred_element_type=jnp.float32)
        masked = jnp.where(allowed[None], scores, NEGATIVE)
        row_top = jnp.max(masked, axis=2, keepdims=True)
        exponent = jnp.where(allowed[None], jnp.exp(masked - row_top), 0.0)
        denominator = jnp.sum(exponent, axis=2)
        numerator = jnp.einsum(
            "hqk,khd->qhd",
            exponent.astype(jnp.bfloat16),
            value_all,
            preferred_element_type=jnp.float32,
        )
        return (numerator / denominator.T[:, :, None]).astype(jnp.bfloat16)

    block_starts = jnp.arange(block_count, dtype=jnp.int32) * block_len
    heads_out = lax.map(query_block, block_starts).reshape(group_len, head_width)
    attn_rows = lax.psum_scatter(
        jnp.dot(heads_out, out_weight, preferred_element_type=jnp.float32).astype(jnp.bfloat16),
        "head",
        scatter_dimension=0,
        tiled=True,
    ).astype(jnp.float32)
    stream = (tokens.astype(jnp.float32) + attn_rows).reshape(local_rows // 4, 4, D)
    average = jnp.sum(stream, axis=2, keepdims=True) / D
    variance = jnp.sum(stream * stream, axis=2, keepdims=True) / D - average * average
    window_rows = ((stream - average) * lax.rsqrt(variance + EPSILON) * merge_gain).astype(
        jnp.bfloat16
    )
    merged_slice = lax.all_to_all(
        window_rows.reshape(local_rows // 4, 4 * D), "head", split_axis=1, concat_axis=0, tiled=True
    )
    merged_count = local_rows // 4
    slot_count = max(2, 2 * merged_count // tok_count)
    owner_col = owners[:, 0]
    owner_hot = (owner_col[:, None] == jnp.arange(tok_count, dtype=jnp.int32)[None, :]).astype(
        jnp.int32
    )
    earlier = jnp.cumsum(owner_hot, axis=0, dtype=jnp.int32) - owner_hot
    slot_index = jnp.sum(earlier * owner_hot, axis=1, dtype=jnp.int32)
    target = owner_col * slot_count + slot_index
    select = (
        jnp.arange(tok_count * slot_count, dtype=jnp.int32)[:, None] == target[None, :]
    ).astype(jnp.bfloat16)
    local_cols = merge_weight.shape[1]
    chunk_cols = local_cols // CHUNKS
    pieces = []
    for chunk in range(CHUNKS):
        weight_part = lax.all_gather(
            merge_weight[:, chunk * chunk_cols : (chunk + 1) * chunk_cols], "tok", axis=1, tiled=True
        )
        column_terms = jnp.dot(merged_slice, weight_part, preferred_element_type=jnp.float32)
        projected = lax.psum_scatter(
            column_terms.astype(jnp.bfloat16), "head", scatter_dimension=0, tiled=True
        )
        send_rows = jnp.dot(select, projected, preferred_element_type=jnp.float32).astype(
            jnp.bfloat16
        )
        send_rows = send_rows.reshape(tok_count, slot_count, -1)
        received = lax.all_to_all(send_rows, "tok", split_axis=0, concat_axis=0, tiled=True)
        pieces.append(received.reshape(tok_count * slot_count, tok_count, 1, chunk_cols))
    received = jnp.concatenate(pieces, axis=2)
    return received.reshape(tok_count * slot_count, -1)


def solution(mesh):
    placed = (
        P(("tok", "head"), None),
        P(),
        P(None, "head", None),
        P("head", None),
        P(),
        P("head", "tok"),
        P(None, "tok"),
        P("tok"),
        P(None, "tok"),
        P("tok"),
        P(("tok", "head"), None),
    )
    return jax.shard_map(
        body, mesh=mesh, in_specs=placed, out_specs=P(("tok", "head"), None), check_vma=False
    )
```

```python
import jax
import jax.numpy as jnp
from jax import lax
from jax.sharding import PartitionSpec as P

D = 1664
HD = 104
SIDE = 16
TOK = ("tx", "tz")
HEAD = ("hy", "hc")
Z_SIZE = 8


EPSILON = 1e-06
NEGATIVE = -1e30


def layer_norm(values, gain_vec):
    average = jnp.mean(values, axis=-1, keepdims=True)
    centred = values - average
    variance = jnp.mean(centred * centred, axis=-1, keepdims=True)
    return centred * lax.rsqrt(variance + EPSILON) * gain_vec


def rotate(vectors, row_coord, col_coord):
    quarter = vectors.shape[-1] // 4
    frequency = 10000.0 ** (-jnp.arange(quarter, dtype=jnp.float32) / quarter)
    pieces = []
    for which_axis, coordinate in ((0, row_coord), (1, col_coord)):
        leading = vectors[..., 2 * which_axis * quarter : (2 * which_axis + 1) * quarter]
        trailing = vectors[..., (2 * which_axis + 1) * quarter : (2 * which_axis + 2) * quarter]
        angles = coordinate[:, None, None] * frequency
        cosine = jnp.cos(angles)
        sine_val = jnp.sin(angles)
        pieces.append(leading * cosine - trailing * sine_val)
        pieces.append(leading * sine_val + trailing * cosine)
    return jnp.concatenate(pieces, axis=-1)


def body(
    tokens,
    attn_gain,
    qkv_weight,
    out_weight,
    merge_gain,
    merge_weight,
    grid_sizes,
    segment_ids,
    patch_pos,
    live_mask,
    owners,
):
    group_len = segment_ids.shape[0]
    local_rows = tokens.shape[0]
    head_width = qkv_weight.shape[1]
    heads_here = head_width // HD
    tok_count = lax.axis_size("tx") * lax.axis_size("tz")
    image_count = grid_sizes.shape[1]
    local_image = segment_ids - (lax.axis_index("tx") * lax.axis_size("tz") + lax.axis_index("tz")) * image_count
    image_match = local_image[:, None] == jnp.arange(image_count, dtype=jnp.int32)[None, :]
    grid_float = grid_sizes.astype(jnp.float32)
    row_size = jnp.sum(jnp.where(image_match, grid_float[0][None, :], 0.0), axis=1)
    col_size = jnp.sum(jnp.where(image_match, grid_float[1][None, :], 0.0), axis=1)
    row_coord = patch_pos[0].astype(jnp.float32) * SIDE / row_size
    col_coord = patch_pos[1].astype(jnp.float32) * SIDE / col_size
    stacked_weight = qkv_weight.reshape(3 * head_width, D)
    normed = layer_norm(tokens.astype(jnp.float32), attn_gain).astype(jnp.bfloat16)
    projected_rows = lax.dot_general(
        lax.all_gather(normed, HEAD, axis=0, tiled=True),
        stacked_weight,
        (((1,), (1,)), ((), ())),
        preferred_element_type=jnp.float32,
    )
    projected_rows = projected_rows.reshape(group_len, 3, heads_here, HD)
    query_all = (rotate(projected_rows[:, 0], row_coord, col_coord) * HD ** (-0.5)).astype(
        jnp.bfloat16
    )
    key_all = rotate(projected_rows[:, 1], row_coord, col_coord).astype(jnp.bfloat16)
    value_all = projected_rows[:, 2].astype(jnp.bfloat16)
    block_len = min(512, group_len)
    block_count = group_len // block_len
    key_live = live_mask == 1

    def allowed_pairs(query_start, span):
        query_seg = lax.dynamic_slice_in_dim(segment_ids, query_start, block_len)
        query_place = query_start + jnp.arange(block_len, dtype=jnp.int32)
        key_place = jnp.arange(span, dtype=jnp.int32)
        same_image = query_seg[:, None] == segment_ids[None, :]
        return same_image & (key_live[None, :] | (query_place[:, None] == key_place[None, :]))

    def query_block(query_start):
        queries = lax.dynamic_slice_in_dim(query_all, query_start, block_len, 0)
        allowed = allowed_pairs(query_start, group_len)
        scores = jnp.einsum("qhd,khd->hqk", queries, key_all, preferred_element_type=jnp.float32)
        masked = jnp.where(allowed[None], scores, NEGATIVE)
        row_top = jnp.max(masked, axis=2, keepdims=True)
        exponent = jnp.where(allowed[None], jnp.exp(masked - row_top), 0.0)
        denominator = jnp.sum(exponent, axis=2)
        numerator = jnp.einsum(
            "hqk,khd->qhd",
            exponent.astype(jnp.bfloat16),
            value_all,
            preferred_element_type=jnp.float32,
        )
        return (numerator / denominator.T[:, :, None]).astype(jnp.bfloat16)

    block_starts = jnp.arange(block_count, dtype=jnp.int32) * block_len
    heads_out = lax.map(query_block, block_starts).reshape(group_len, head_width)
    attn_rows = lax.psum_scatter(
        jnp.dot(heads_out, out_weight, preferred_element_type=jnp.float32).astype(jnp.bfloat16),
        HEAD,
        scatter_dimension=0,
        tiled=True,
    ).astype(jnp.float32)
    stream = (tokens.astype(jnp.float32) + attn_rows).reshape(local_rows // 4, 4, D)
    average = jnp.sum(stream, axis=2, keepdims=True) / D
    variance = jnp.sum(stream * stream, axis=2, keepdims=True) / D - average * average
    window_rows = ((stream - average) * lax.rsqrt(variance + EPSILON) * merge_gain).astype(
        jnp.bfloat16
    )
    merged_slice = lax.all_to_all(
        window_rows.reshape(local_rows // 4, 4 * D), HEAD, split_axis=1, concat_axis=0, tiled=True
    )
    merged_count = local_rows // 4
    column_terms = jnp.dot(
        merged_slice,
        lax.all_gather(
            lax.all_gather(merge_weight, "tz", axis=1, tiled=True), "tx", axis=1, tiled=True
        ),
        preferred_element_type=jnp.float32,
    )
    projected = lax.psum_scatter(
        column_terms.astype(jnp.bfloat16), HEAD, scatter_dimension=0, tiled=True
    )
    slot_count = max(2, 2 * merged_count // tok_count)
    owner_col = owners[:, 0]
    owner_hot = (owner_col[:, None] == jnp.arange(tok_count, dtype=jnp.int32)[None, :]).astype(
        jnp.int32
    )
    earlier = jnp.cumsum(owner_hot, axis=0, dtype=jnp.int32) - owner_hot
    slot_index = jnp.sum(earlier * owner_hot, axis=1, dtype=jnp.int32)
    target = owner_col * slot_count + slot_index
    select = (
        jnp.arange(tok_count * slot_count, dtype=jnp.int32)[:, None] == target[None, :]
    ).astype(jnp.bfloat16)
    send_rows = jnp.dot(select, projected, preferred_element_type=jnp.float32).astype(jnp.bfloat16)
    send_rows = send_rows.reshape(tok_count, slot_count, -1)
    received = lax.all_to_all(send_rows, TOK, split_axis=0, concat_axis=0, tiled=True)
    return received.reshape(tok_count * slot_count, -1)


def solution(mesh):
    tok_size, head_size = (mesh.shape[name] for name in mesh.axis_names)
    split_mesh = jax.sharding.Mesh(
        mesh.devices.reshape(tok_size // Z_SIZE, Z_SIZE, head_size // 2, 2), TOK + HEAD
    )
    placed = (
        P(TOK + HEAD, None),
        P(),
        P(None, HEAD, None),
        P(HEAD, None),
        P(),
        P(HEAD, TOK),
        P(None, TOK),
        P(TOK),
        P(None, TOK),
        P(TOK),
        P(TOK + HEAD, None),
    )
    return jax.shard_map(
        body, mesh=split_mesh, in_specs=placed, out_specs=P(TOK + HEAD, None), check_vma=False
    )
```

```python
import jax
import jax.numpy as jnp
from jax import lax
from jax.sharding import PartitionSpec as P

D = 1664
HD = 104
SIDE = 16


EPSILON = 1e-06
NEGATIVE = -1e30


def layer_norm(values, gain_vec):
    average = jnp.mean(values, axis=-1, keepdims=True)
    centred = values - average
    variance = jnp.mean(centred * centred, axis=-1, keepdims=True)
    return centred * lax.rsqrt(variance + EPSILON) * gain_vec


def rotate(vectors, row_coord, col_coord):
    quarter = vectors.shape[-1] // 4
    frequency = 10000.0 ** (-jnp.arange(quarter, dtype=jnp.float32) / quarter)
    pieces = []
    for which_axis, coordinate in ((0, row_coord), (1, col_coord)):
        leading = vectors[..., 2 * which_axis * quarter : (2 * which_axis + 1) * quarter]
        trailing = vectors[..., (2 * which_axis + 1) * quarter : (2 * which_axis + 2) * quarter]
        angles = coordinate[:, None, None] * frequency
        cosine = jnp.cos(angles)
        sine_val = jnp.sin(angles)
        pieces.append(leading * cosine - trailing * sine_val)
        pieces.append(leading * sine_val + trailing * cosine)
    return jnp.concatenate(pieces, axis=-1)


def body(
    tokens,
    attn_gain,
    qkv_weight,
    out_weight,
    merge_gain,
    merge_weight,
    grid_sizes,
    segment_ids,
    patch_pos,
    live_mask,
    owners,
):
    group_len = segment_ids.shape[0]
    local_rows = tokens.shape[0]
    head_width = qkv_weight.shape[1]
    heads_here = head_width // HD
    tok_count = lax.axis_size("tok")
    image_count = grid_sizes.shape[1]
    local_image = segment_ids - lax.axis_index("tok") * image_count
    image_match = local_image[:, None] == jnp.arange(image_count, dtype=jnp.int32)[None, :]
    grid_float = grid_sizes.astype(jnp.float32)
    row_size = jnp.sum(jnp.where(image_match, grid_float[0][None, :], 0.0), axis=1)
    col_size = jnp.sum(jnp.where(image_match, grid_float[1][None, :], 0.0), axis=1)
    row_coord = patch_pos[0].astype(jnp.float32) * SIDE / row_size
    col_coord = patch_pos[1].astype(jnp.float32) * SIDE / col_size
    stacked_weight = qkv_weight.reshape(3 * head_width, D)
    normed = layer_norm(tokens.astype(jnp.float32), attn_gain).astype(jnp.bfloat16)
    full_merge_weight = lax.all_gather(merge_weight, "tok", axis=1, tiled=True)
    projected_rows = lax.dot_general(
        lax.all_gather(normed, "head", axis=0, tiled=True),
        stacked_weight,
        (((1,), (1,)), ((), ())),
        preferred_element_type=jnp.float32,
    )
    projected_rows = projected_rows.reshape(group_len, 3, heads_here, HD)
    query_all = (rotate(projected_rows[:, 0], row_coord, col_coord) * HD ** (-0.5)).astype(
        jnp.bfloat16
    )
    key_all = rotate(projected_rows[:, 1], row_coord, col_coord).astype(jnp.bfloat16)
    value_all = projected_rows[:, 2].astype(jnp.bfloat16)
    block_len = min(512, group_len)
    block_count = group_len // block_len
    key_live = live_mask == 1

    def allowed_pairs(query_start, span):
        query_seg = lax.dynamic_slice_in_dim(segment_ids, query_start, block_len)
        query_place = query_start + jnp.arange(block_len, dtype=jnp.int32)
        key_place = jnp.arange(span, dtype=jnp.int32)
        same_image = query_seg[:, None] == segment_ids[None, :]
        return same_image & (key_live[None, :] | (query_place[:, None] == key_place[None, :]))

    def query_block(query_start):
        queries = lax.dynamic_slice_in_dim(query_all, query_start, block_len, 0)
        allowed = allowed_pairs(query_start, group_len)
        scores = jnp.einsum("qhd,khd->hqk", queries, key_all, preferred_element_type=jnp.float32)
        masked = jnp.where(allowed[None], scores, NEGATIVE)
        row_top = jnp.max(masked, axis=2, keepdims=True)
        exponent = jnp.where(allowed[None], jnp.exp(masked - row_top), 0.0)
        denominator = jnp.sum(exponent, axis=2)
        numerator = jnp.einsum(
            "hqk,khd->qhd",
            exponent.astype(jnp.bfloat16),
            value_all,
            preferred_element_type=jnp.float32,
        )
        return (numerator / denominator.T[:, :, None]).astype(jnp.bfloat16)

    block_starts = jnp.arange(block_count, dtype=jnp.int32) * block_len
    heads_out = lax.map(query_block, block_starts).reshape(group_len, head_width)
    head_count = lax.axis_size("head")
    head_terms = jnp.dot(heads_out, out_weight, preferred_element_type=jnp.float32).astype(
        jnp.bfloat16
    )
    head_terms = lax.all_to_all(
        head_terms.reshape(head_count, local_rows, D), "head", split_axis=0, concat_axis=0, tiled=True
    )
    attn_rows = jnp.sum(head_terms.astype(jnp.float32), axis=0)
    stream = (tokens.astype(jnp.float32) + attn_rows).reshape(local_rows // 4, 4, D)
    average = jnp.sum(stream, axis=2, keepdims=True) / D
    variance = jnp.sum(stream * stream, axis=2, keepdims=True) / D - average * average
    window_rows = ((stream - average) * lax.rsqrt(variance + EPSILON) * merge_gain).astype(
        jnp.bfloat16
    )
    merged_slice = lax.all_to_all(
        window_rows.reshape(local_rows // 4, 4 * D), "head", split_axis=1, concat_axis=0, tiled=True
    )
    merged_count = local_rows // 4
    column_terms = jnp.dot(
        merged_slice,
        full_merge_weight,
        preferred_element_type=jnp.float32,
    )
    projected = lax.psum_scatter(
        column_terms.astype(jnp.bfloat16), "head", scatter_dimension=0, tiled=True
    )
    slot_count = max(2, 2 * merged_count // tok_count)
    owner_col = owners[:, 0]
    owner_hot = (owner_col[:, None] == jnp.arange(tok_count, dtype=jnp.int32)[None, :]).astype(
        jnp.int32
    )
    earlier = jnp.cumsum(owner_hot, axis=0, dtype=jnp.int32) - owner_hot
    slot_index = jnp.sum(earlier * owner_hot, axis=1, dtype=jnp.int32)
    target = owner_col * slot_count + slot_index
    select = (
        jnp.arange(tok_count * slot_count, dtype=jnp.int32)[:, None] == target[None, :]
    ).astype(jnp.bfloat16)
    send_rows = jnp.dot(select, projected, preferred_element_type=jnp.float32).astype(jnp.bfloat16)
    send_rows = send_rows.reshape(tok_count, slot_count, -1)
    received = lax.all_to_all(send_rows, "tok", split_axis=0, concat_axis=0, tiled=True)
    return received.reshape(tok_count * slot_count, -1)


def solution(mesh):
    placed = (
        P(("tok", "head"), None),
        P(),
        P(None, "head", None),
        P("head", None),
        P(),
        P("head", "tok"),
        P(None, "tok"),
        P("tok"),
        P(None, "tok"),
        P("tok"),
        P(("tok", "head"), None),
    )
    return jax.shard_map(
        body, mesh=mesh, in_specs=placed, out_specs=P(("tok", "head"), None), check_vma=False
    )
```

```python
import jax
import jax.numpy as jnp
from jax import lax
from jax.sharding import PartitionSpec as P

D = 1664
HD = 104
SIDE = 16
QUERY_PARTS = 2


EPSILON = 1e-06
NEGATIVE = -1e30


def layer_norm(values, gain_vec):
    average = jnp.mean(values, axis=-1, keepdims=True)
    centred = values - average
    variance = jnp.mean(centred * centred, axis=-1, keepdims=True)
    return centred * lax.rsqrt(variance + EPSILON) * gain_vec


def rotate(vectors, row_coord, col_coord):
    quarter = vectors.shape[-1] // 4
    frequency = 10000.0 ** (-jnp.arange(quarter, dtype=jnp.float32) / quarter)
    pieces = []
    for which_axis, coordinate in ((0, row_coord), (1, col_coord)):
        leading = vectors[..., 2 * which_axis * quarter : (2 * which_axis + 1) * quarter]
        trailing = vectors[..., (2 * which_axis + 1) * quarter : (2 * which_axis + 2) * quarter]
        angles = coordinate[:, None, None] * frequency
        cosine = jnp.cos(angles)
        sine_val = jnp.sin(angles)
        pieces.append(leading * cosine - trailing * sine_val)
        pieces.append(leading * sine_val + trailing * cosine)
    return jnp.concatenate(pieces, axis=-1)


def body(
    tokens,
    attn_gain,
    qkv_weight,
    out_weight,
    merge_gain,
    merge_weight,
    grid_sizes,
    segment_ids,
    patch_pos,
    live_mask,
    owners,
):
    group_len = segment_ids.shape[0]
    local_rows = tokens.shape[0]
    head_width = qkv_weight.shape[1]
    heads_here = head_width // HD
    tok_count = lax.axis_size("tok")
    image_count = grid_sizes.shape[1]
    local_image = segment_ids - lax.axis_index("tok") * image_count
    image_match = local_image[:, None] == jnp.arange(image_count, dtype=jnp.int32)[None, :]
    grid_float = grid_sizes.astype(jnp.float32)
    row_size = jnp.sum(jnp.where(image_match, grid_float[0][None, :], 0.0), axis=1)
    col_size = jnp.sum(jnp.where(image_match, grid_float[1][None, :], 0.0), axis=1)
    row_coord = patch_pos[0].astype(jnp.float32) * SIDE / row_size
    col_coord = patch_pos[1].astype(jnp.float32) * SIDE / col_size
    stacked_weight = qkv_weight.reshape(3 * head_width, D)
    normed = layer_norm(tokens.astype(jnp.float32), attn_gain).astype(jnp.bfloat16)
    full_merge_weight = lax.all_gather(merge_weight, "tok", axis=1, tiled=True)
    projected_rows = lax.dot_general(
        lax.all_gather(normed, "head", axis=0, tiled=True),
        stacked_weight,
        (((1,), (1,)), ((), ())),
        preferred_element_type=jnp.float32,
    )
    projected_rows = projected_rows.reshape(group_len, 3, heads_here, HD)
    query_all = (rotate(projected_rows[:, 0], row_coord, col_coord) * HD ** (-0.5)).astype(
        jnp.bfloat16
    )
    key_all = rotate(projected_rows[:, 1], row_coord, col_coord).astype(jnp.bfloat16)
    value_all = projected_rows[:, 2].astype(jnp.bfloat16)
    key_live = live_mask == 1

    head_count = lax.axis_size("head")
    key_live = live_mask == 1
    part_rows = local_rows // QUERY_PARTS
    attn_parts = []
    for part in range(QUERY_PARTS):
        picked = lambda values: values.reshape(
            (head_count, QUERY_PARTS, part_rows) + values.shape[1:]
        )[:, part].reshape((head_count * part_rows,) + values.shape[1:])
        queries = picked(query_all)
        query_seg = picked(segment_ids)
        query_place = picked(jnp.arange(group_len, dtype=jnp.int32))
        key_place = jnp.arange(group_len, dtype=jnp.int32)
        same_image = query_seg[:, None] == segment_ids[None, :]
        allowed = same_image & (key_live[None, :] | (query_place[:, None] == key_place[None, :]))
        scores = jnp.einsum("qhd,khd->hqk", queries, key_all, preferred_element_type=jnp.float32)
        masked = jnp.where(allowed[None], scores, NEGATIVE)
        row_top = jnp.max(masked, axis=2, keepdims=True)
        exponent = jnp.where(allowed[None], jnp.exp(masked - row_top), 0.0)
        denominator = jnp.sum(exponent, axis=2)
        numerator = jnp.einsum(
            "hqk,khd->qhd",
            exponent.astype(jnp.bfloat16),
            value_all,
            preferred_element_type=jnp.float32,
        )
        part_out = (numerator / denominator.T[:, :, None]).astype(jnp.bfloat16)
        part_terms = jnp.dot(
            part_out.reshape(head_count * part_rows, head_width),
            out_weight,
            preferred_element_type=jnp.float32,
        ).astype(jnp.bfloat16)
        part_terms = lax.all_to_all(
            part_terms.reshape(head_count, part_rows, D), "head", split_axis=0, concat_axis=0, tiled=True
        )
        attn_parts.append(jnp.sum(part_terms.astype(jnp.float32), axis=0))
    attn_rows = jnp.concatenate(attn_parts, axis=0)
    stream = (tokens.astype(jnp.float32) + attn_rows).reshape(local_rows // 4, 4, D)
    average = jnp.sum(stream, axis=2, keepdims=True) / D
    variance = jnp.sum(stream * stream, axis=2, keepdims=True) / D - average * average
    window_rows = ((stream - average) * lax.rsqrt(variance + EPSILON) * merge_gain).astype(
        jnp.bfloat16
    )
    merged_slice = lax.all_to_all(
        window_rows.reshape(local_rows // 4, 4 * D), "head", split_axis=1, concat_axis=0, tiled=True
    )
    merged_count = local_rows // 4
    column_terms = jnp.dot(
        merged_slice,
        full_merge_weight,
        preferred_element_type=jnp.float32,
    )
    column_terms = lax.all_to_all(
        column_terms.astype(jnp.bfloat16).reshape(head_count, merged_count, -1),
        "head",
        split_axis=0,
        concat_axis=0,
        tiled=True,
    )
    projected = jnp.sum(column_terms.astype(jnp.float32), axis=0).astype(jnp.bfloat16)
    slot_count = max(2, 2 * merged_count // tok_count)
    owner_col = owners[:, 0]
    owner_hot = (owner_col[:, None] == jnp.arange(tok_count, dtype=jnp.int32)[None, :]).astype(
        jnp.int32
    )
    earlier = jnp.cumsum(owner_hot, axis=0, dtype=jnp.int32) - owner_hot
    slot_index = jnp.sum(earlier * owner_hot, axis=1, dtype=jnp.int32)
    target = owner_col * slot_count + slot_index
    select = (
        jnp.arange(tok_count * slot_count, dtype=jnp.int32)[:, None] == target[None, :]
    ).astype(jnp.bfloat16)
    send_rows = jnp.dot(select, projected, preferred_element_type=jnp.float32).astype(jnp.bfloat16)
    send_rows = send_rows.reshape(tok_count, slot_count, -1)
    received = lax.all_to_all(send_rows, "tok", split_axis=0, concat_axis=0, tiled=True)
    return received.reshape(tok_count * slot_count, -1)


def solution(mesh):
    placed = (
        P(("tok", "head"), None),
        P(),
        P(None, "head", None),
        P("head", None),
        P(),
        P("head", "tok"),
        P(None, "tok"),
        P("tok"),
        P(None, "tok"),
        P("tok"),
        P(("tok", "head"), None),
    )
    return jax.shard_map(
        body, mesh=mesh, in_specs=placed, out_specs=P(("tok", "head"), None), check_vma=False
    )
```

```python
import jax
import jax.numpy as jnp
from jax import lax
from jax.sharding import PartitionSpec as P

D = 1664
HD = 104
SIDE = 16


EPSILON = 1e-06
NEGATIVE = -1e30


def layer_norm(values, gain_vec):
    average = jnp.mean(values, axis=-1, keepdims=True)
    centred = values - average
    variance = jnp.mean(centred * centred, axis=-1, keepdims=True)
    return centred * lax.rsqrt(variance + EPSILON) * gain_vec


def rotate(vectors, row_coord, col_coord):
    quarter = vectors.shape[-1] // 4
    frequency = 10000.0 ** (-jnp.arange(quarter, dtype=jnp.float32) / quarter)
    pieces = []
    for which_axis, coordinate in ((0, row_coord), (1, col_coord)):
        leading = vectors[..., 2 * which_axis * quarter : (2 * which_axis + 1) * quarter]
        trailing = vectors[..., (2 * which_axis + 1) * quarter : (2 * which_axis + 2) * quarter]
        angles = coordinate[:, None, None] * frequency
        cosine = jnp.cos(angles)
        sine_val = jnp.sin(angles)
        pieces.append(leading * cosine - trailing * sine_val)
        pieces.append(leading * sine_val + trailing * cosine)
    return jnp.concatenate(pieces, axis=-1)


def body(
    tokens,
    attn_gain,
    qkv_weight,
    out_weight,
    merge_gain,
    merge_weight,
    grid_sizes,
    segment_ids,
    patch_pos,
    live_mask,
    owners,
):
    group_len = segment_ids.shape[0]
    local_rows = tokens.shape[0]
    head_width = qkv_weight.shape[1]
    heads_here = head_width // HD
    tok_count = lax.axis_size("tok")
    image_count = grid_sizes.shape[1]
    local_image = segment_ids - lax.axis_index("tok") * image_count
    image_match = local_image[:, None] == jnp.arange(image_count, dtype=jnp.int32)[None, :]
    grid_float = grid_sizes.astype(jnp.float32)
    row_size = jnp.sum(jnp.where(image_match, grid_float[0][None, :], 0.0), axis=1)
    col_size = jnp.sum(jnp.where(image_match, grid_float[1][None, :], 0.0), axis=1)
    row_coord = patch_pos[0].astype(jnp.float32) * SIDE / row_size
    col_coord = patch_pos[1].astype(jnp.float32) * SIDE / col_size
    stacked_weight = qkv_weight.reshape(3 * head_width, D)
    normed = layer_norm(tokens.astype(jnp.float32), attn_gain).astype(jnp.bfloat16)
    full_merge_weight = lax.all_gather(merge_weight, "tok", axis=1, tiled=True)
    projected_rows = lax.dot_general(
        lax.all_gather(normed, "head", axis=0, tiled=True),
        stacked_weight,
        (((1,), (1,)), ((), ())),
        preferred_element_type=jnp.float32,
    )
    projected_rows = projected_rows.reshape(group_len, 3, heads_here, HD)
    query_all = (rotate(projected_rows[:, 0], row_coord, col_coord) * HD ** (-0.5)).astype(
        jnp.bfloat16
    )
    key_all = rotate(projected_rows[:, 1], row_coord, col_coord).astype(jnp.bfloat16)
    value_all = projected_rows[:, 2].astype(jnp.bfloat16)
    block_len = min(1024, group_len)
    block_count = group_len // block_len
    key_live = live_mask == 1

    def allowed_pairs(query_start, span):
        query_seg = lax.dynamic_slice_in_dim(segment_ids, query_start, block_len)
        query_place = query_start + jnp.arange(block_len, dtype=jnp.int32)
        key_place = jnp.arange(span, dtype=jnp.int32)
        same_image = query_seg[:, None] == segment_ids[None, :]
        return same_image & (key_live[None, :] | (query_place[:, None] == key_place[None, :]))

    def query_block(query_start):
        queries = lax.dynamic_slice_in_dim(query_all, query_start, block_len, 0)
        allowed = allowed_pairs(query_start, group_len)
        scores = jnp.einsum("qhd,khd->hqk", queries, key_all, preferred_element_type=jnp.float32)
        masked = jnp.where(allowed[None], scores, NEGATIVE)
        row_top = jnp.max(masked, axis=2, keepdims=True)
        exponent = jnp.where(allowed[None], jnp.exp(masked - row_top), 0.0)
        denominator = jnp.sum(exponent, axis=2)
        numerator = jnp.einsum(
            "hqk,khd->qhd",
            exponent.astype(jnp.bfloat16),
            value_all,
            preferred_element_type=jnp.float32,
        )
        return (numerator / denominator.T[:, :, None]).astype(jnp.bfloat16)

    block_starts = jnp.arange(block_count, dtype=jnp.int32) * block_len
    heads_out = lax.map(query_block, block_starts).reshape(group_len, head_width)
    head_count = lax.axis_size("head")
    head_terms = jnp.dot(heads_out, out_weight, preferred_element_type=jnp.float32).astype(
        jnp.bfloat16
    )
    head_terms = lax.all_to_all(
        head_terms.reshape(head_count, local_rows, D), "head", split_axis=0, concat_axis=0, tiled=True
    )
    attn_rows = jnp.sum(head_terms.astype(jnp.float32), axis=0)
    stream = (tokens.astype(jnp.float32) + attn_rows).reshape(local_rows // 4, 4, D)
    average = jnp.sum(stream, axis=2, keepdims=True) / D
    variance = jnp.sum(stream * stream, axis=2, keepdims=True) / D - average * average
    window_rows = ((stream - average) * lax.rsqrt(variance + EPSILON) * merge_gain).astype(
        jnp.bfloat16
    )
    merged_slice = lax.all_to_all(
        window_rows.reshape(local_rows // 4, 4 * D), "head", split_axis=1, concat_axis=0, tiled=True
    )
    merged_count = local_rows // 4
    column_terms = jnp.dot(
        merged_slice,
        full_merge_weight,
        preferred_element_type=jnp.float32,
    )
    column_terms = lax.all_to_all(
        column_terms.astype(jnp.bfloat16).reshape(head_count, merged_count, -1),
        "head",
        split_axis=0,
        concat_axis=0,
        tiled=True,
    )
    projected = jnp.sum(column_terms.astype(jnp.float32), axis=0).astype(jnp.bfloat16)
    slot_count = max(2, 2 * merged_count // tok_count)
    owner_col = owners[:, 0]
    owner_hot = (owner_col[:, None] == jnp.arange(tok_count, dtype=jnp.int32)[None, :]).astype(
        jnp.int32
    )
    earlier = jnp.cumsum(owner_hot, axis=0, dtype=jnp.int32) - owner_hot
    slot_index = jnp.sum(earlier * owner_hot, axis=1, dtype=jnp.int32)
    target = owner_col * slot_count + slot_index
    select = (
        jnp.arange(tok_count * slot_count, dtype=jnp.int32)[:, None] == target[None, :]
    ).astype(jnp.bfloat16)
    send_rows = jnp.dot(select, projected, preferred_element_type=jnp.float32).astype(jnp.bfloat16)
    send_rows = send_rows.reshape(tok_count, slot_count, -1)
    received = lax.all_to_all(send_rows, "tok", split_axis=0, concat_axis=0, tiled=True)
    return received.reshape(tok_count * slot_count, -1)


def solution(mesh):
    placed = (
        P(("tok", "head"), None),
        P(),
        P(None, "head", None),
        P("head", None),
        P(),
        P("head", "tok"),
        P(None, "tok"),
        P("tok"),
        P(None, "tok"),
        P("tok"),
        P(("tok", "head"), None),
    )
    return jax.shard_map(
        body, mesh=mesh, in_specs=placed, out_specs=P(("tok", "head"), None), check_vma=False
    )
```

```python
import jax
import jax.numpy as jnp
from jax import lax
from jax.sharding import PartitionSpec as P

D = 1664
HD = 104
SIDE = 16
TOK = ("tx", "tz")
HEAD = ("hy", "hc")
Z_SIZE = 8


EPSILON = 1e-06
NEGATIVE = -1e30


def layer_norm(values, gain_vec):
    average = jnp.mean(values, axis=-1, keepdims=True)
    centred = values - average
    variance = jnp.mean(centred * centred, axis=-1, keepdims=True)
    return centred * lax.rsqrt(variance + EPSILON) * gain_vec


def rotate(vectors, row_coord, col_coord):
    quarter = vectors.shape[-1] // 4
    frequency = 10000.0 ** (-jnp.arange(quarter, dtype=jnp.float32) / quarter)
    pieces = []
    for which_axis, coordinate in ((0, row_coord), (1, col_coord)):
        leading = vectors[..., 2 * which_axis * quarter : (2 * which_axis + 1) * quarter]
        trailing = vectors[..., (2 * which_axis + 1) * quarter : (2 * which_axis + 2) * quarter]
        angles = coordinate[:, None, None] * frequency
        cosine = jnp.cos(angles)
        sine_val = jnp.sin(angles)
        pieces.append(leading * cosine - trailing * sine_val)
        pieces.append(leading * sine_val + trailing * cosine)
    return jnp.concatenate(pieces, axis=-1)


def body(
    tokens,
    attn_gain,
    qkv_weight,
    out_weight,
    merge_gain,
    merge_weight,
    grid_sizes,
    segment_ids,
    patch_pos,
    live_mask,
    owners,
):
    group_len = segment_ids.shape[0]
    local_rows = tokens.shape[0]
    head_width = qkv_weight.shape[1]
    heads_here = head_width // HD
    tok_count = lax.axis_size("tx") * lax.axis_size("tz")
    image_count = grid_sizes.shape[1]
    local_image = segment_ids - (lax.axis_index("tx") * lax.axis_size("tz") + lax.axis_index("tz")) * image_count
    image_match = local_image[:, None] == jnp.arange(image_count, dtype=jnp.int32)[None, :]
    grid_float = grid_sizes.astype(jnp.float32)
    row_size = jnp.sum(jnp.where(image_match, grid_float[0][None, :], 0.0), axis=1)
    col_size = jnp.sum(jnp.where(image_match, grid_float[1][None, :], 0.0), axis=1)
    row_coord = patch_pos[0].astype(jnp.float32) * SIDE / row_size
    col_coord = patch_pos[1].astype(jnp.float32) * SIDE / col_size
    stacked_weight = qkv_weight.reshape(3 * head_width, D)
    normed = layer_norm(tokens.astype(jnp.float32), attn_gain).astype(jnp.bfloat16)
    full_merge_weight = lax.all_gather(merge_weight, TOK, axis=1, tiled=True)
    projected_rows = lax.dot_general(
        lax.all_gather(normed, HEAD, axis=0, tiled=True),
        stacked_weight,
        (((1,), (1,)), ((), ())),
        preferred_element_type=jnp.float32,
    )
    projected_rows = projected_rows.reshape(group_len, 3, heads_here, HD)
    query_all = (rotate(projected_rows[:, 0], row_coord, col_coord) * HD ** (-0.5)).astype(
        jnp.bfloat16
    )
    key_all = rotate(projected_rows[:, 1], row_coord, col_coord).astype(jnp.bfloat16)
    value_all = projected_rows[:, 2].astype(jnp.bfloat16)
    block_len = min(1024, group_len)
    block_count = group_len // block_len
    key_live = live_mask == 1

    def allowed_pairs(query_start, span):
        query_seg = lax.dynamic_slice_in_dim(segment_ids, query_start, block_len)
        query_place = query_start + jnp.arange(block_len, dtype=jnp.int32)
        key_place = jnp.arange(span, dtype=jnp.int32)
        same_image = query_seg[:, None] == segment_ids[None, :]
        return same_image & (key_live[None, :] | (query_place[:, None] == key_place[None, :]))

    def query_block(query_start):
        queries = lax.dynamic_slice_in_dim(query_all, query_start, block_len, 0)
        allowed = allowed_pairs(query_start, group_len)
        scores = jnp.einsum("qhd,khd->hqk", queries, key_all, preferred_element_type=jnp.float32)
        masked = jnp.where(allowed[None], scores, NEGATIVE)
        row_top = jnp.max(masked, axis=2, keepdims=True)
        exponent = jnp.where(allowed[None], jnp.exp(masked - row_top), 0.0)
        denominator = jnp.sum(exponent, axis=2)
        numerator = jnp.einsum(
            "hqk,khd->qhd",
            exponent.astype(jnp.bfloat16),
            value_all,
            preferred_element_type=jnp.float32,
        )
        return (numerator / denominator.T[:, :, None]).astype(jnp.bfloat16)

    block_starts = jnp.arange(block_count, dtype=jnp.int32) * block_len
    heads_out = lax.map(query_block, block_starts).reshape(group_len, head_width)
    head_count = lax.axis_size(HEAD)
    head_terms = jnp.dot(heads_out, out_weight, preferred_element_type=jnp.float32).astype(
        jnp.bfloat16
    )
    head_terms = lax.all_to_all(
        head_terms.reshape(head_count, local_rows, D), HEAD, split_axis=0, concat_axis=0, tiled=True
    )
    attn_rows = jnp.sum(head_terms.astype(jnp.float32), axis=0)
    stream = (tokens.astype(jnp.float32) + attn_rows).reshape(local_rows // 4, 4, D)
    average = jnp.sum(stream, axis=2, keepdims=True) / D
    variance = jnp.sum(stream * stream, axis=2, keepdims=True) / D - average * average
    window_rows = ((stream - average) * lax.rsqrt(variance + EPSILON) * merge_gain).astype(
        jnp.bfloat16
    )
    merged_slice = lax.all_to_all(
        window_rows.reshape(local_rows // 4, 4 * D), HEAD, split_axis=1, concat_axis=0, tiled=True
    )
    merged_count = local_rows // 4
    column_terms = jnp.dot(
        merged_slice,
        full_merge_weight,
        preferred_element_type=jnp.float32,
    )
    column_terms = lax.all_to_all(
        column_terms.astype(jnp.bfloat16).reshape(head_count, merged_count, -1),
        HEAD,
        split_axis=0,
        concat_axis=0,
        tiled=True,
    )
    projected = jnp.sum(column_terms.astype(jnp.float32), axis=0).astype(jnp.bfloat16)
    slot_count = max(2, 2 * merged_count // tok_count)
    owner_col = owners[:, 0]
    owner_hot = (owner_col[:, None] == jnp.arange(tok_count, dtype=jnp.int32)[None, :]).astype(
        jnp.int32
    )
    earlier = jnp.cumsum(owner_hot, axis=0, dtype=jnp.int32) - owner_hot
    slot_index = jnp.sum(earlier * owner_hot, axis=1, dtype=jnp.int32)
    x_count = lax.axis_size("tx")
    z_count = lax.axis_size("tz")
    owner_x = owner_col // z_count
    owner_z = owner_col % z_count
    target = (owner_z * x_count + owner_x) * slot_count + slot_index
    select = (
        jnp.arange(tok_count * slot_count, dtype=jnp.int32)[:, None] == target[None, :]
    ).astype(jnp.bfloat16)
    send_rows = jnp.dot(select, projected, preferred_element_type=jnp.float32).astype(jnp.bfloat16)
    send_rows = send_rows.reshape(z_count, x_count, slot_count, -1)
    by_z = lax.all_to_all(send_rows, "tz", split_axis=0, concat_axis=0, tiled=True)
    by_z = jnp.swapaxes(by_z, 0, 1)
    received = lax.all_to_all(by_z, "tx", split_axis=0, concat_axis=0, tiled=True)
    return received.reshape(tok_count * slot_count, -1)


def solution(mesh):
    tok_size, head_size = (mesh.shape[name] for name in mesh.axis_names)
    split_mesh = jax.sharding.Mesh(
        mesh.devices.reshape(tok_size // Z_SIZE, Z_SIZE, head_size // 2, 2), TOK + HEAD
    )
    placed = (
        P(TOK + HEAD, None),
        P(),
        P(None, HEAD, None),
        P(HEAD, None),
        P(),
        P(HEAD, TOK),
        P(None, TOK),
        P(TOK),
        P(None, TOK),
        P(TOK),
        P(TOK + HEAD, None),
    )
    return jax.shard_map(
        body, mesh=split_mesh, in_specs=placed, out_specs=P(TOK + HEAD, None), check_vma=False
    )
```

```python
import jax
import jax.numpy as jnp
from jax import lax
from jax.sharding import PartitionSpec as P

D = 1664
HD = 104
SIDE = 16


EPSILON = 1e-06
NEGATIVE = -1e30


def layer_norm(values, gain_vec):
    average = jnp.mean(values, axis=-1, keepdims=True)
    centred = values - average
    variance = jnp.mean(centred * centred, axis=-1, keepdims=True)
    return centred * lax.rsqrt(variance + EPSILON) * gain_vec


def rotate(vectors, row_coord, col_coord):
    quarter = vectors.shape[-1] // 4
    frequency = 10000.0 ** (-jnp.arange(quarter, dtype=jnp.float32) / quarter)
    pieces = []
    for which_axis, coordinate in ((0, row_coord), (1, col_coord)):
        leading = vectors[..., 2 * which_axis * quarter : (2 * which_axis + 1) * quarter]
        trailing = vectors[..., (2 * which_axis + 1) * quarter : (2 * which_axis + 2) * quarter]
        angles = coordinate[:, None, None] * frequency
        cosine = jnp.cos(angles)
        sine_val = jnp.sin(angles)
        pieces.append(leading * cosine - trailing * sine_val)
        pieces.append(leading * sine_val + trailing * cosine)
    return jnp.concatenate(pieces, axis=-1)


def body(
    tokens,
    attn_gain,
    qkv_weight,
    out_weight,
    merge_gain,
    merge_weight,
    grid_sizes,
    segment_ids,
    patch_pos,
    live_mask,
    owners,
):
    group_len = segment_ids.shape[0]
    local_rows = tokens.shape[0]
    head_width = qkv_weight.shape[1]
    heads_here = head_width // HD
    tok_count = lax.axis_size("tok")
    image_count = grid_sizes.shape[1]
    local_image = segment_ids - lax.axis_index("tok") * image_count
    image_match = local_image[:, None] == jnp.arange(image_count, dtype=jnp.int32)[None, :]
    grid_float = grid_sizes.astype(jnp.float32)
    row_size = jnp.sum(jnp.where(image_match, grid_float[0][None, :], 0.0), axis=1)
    col_size = jnp.sum(jnp.where(image_match, grid_float[1][None, :], 0.0), axis=1)
    row_coord = patch_pos[0].astype(jnp.float32) * SIDE / row_size
    col_coord = patch_pos[1].astype(jnp.float32) * SIDE / col_size
    stacked_weight = qkv_weight.reshape(3 * head_width, D)
    full_merge_weight = lax.all_gather(merge_weight, "tok", axis=1, tiled=True)
    projected_rows = lax.dot_general(
        layer_norm(
            lax.all_gather(tokens, "head", axis=0, tiled=True).astype(jnp.float32), attn_gain
        ).astype(jnp.bfloat16),
        stacked_weight,
        (((1,), (1,)), ((), ())),
        preferred_element_type=jnp.float32,
    )
    projected_rows = projected_rows.reshape(group_len, 3, heads_here, HD)
    query_all = (rotate(projected_rows[:, 0], row_coord, col_coord) * HD ** (-0.5)).astype(
        jnp.bfloat16
    )
    key_all = rotate(projected_rows[:, 1], row_coord, col_coord).astype(jnp.bfloat16)
    value_all = projected_rows[:, 2].astype(jnp.bfloat16)
    block_len = min(1024, group_len)
    block_count = group_len // block_len
    key_live = live_mask == 1

    def allowed_pairs(query_start, span):
        query_seg = lax.dynamic_slice_in_dim(segment_ids, query_start, block_len)
        query_place = query_start + jnp.arange(block_len, dtype=jnp.int32)
        key_place = jnp.arange(span, dtype=jnp.int32)
        same_image = query_seg[:, None] == segment_ids[None, :]
        return same_image & (key_live[None, :] | (query_place[:, None] == key_place[None, :]))

    def query_block(query_start):
        queries = lax.dynamic_slice_in_dim(query_all, query_start, block_len, 0)
        allowed = allowed_pairs(query_start, group_len)
        scores = jnp.einsum("qhd,khd->hqk", queries, key_all, preferred_element_type=jnp.float32)
        masked = jnp.where(allowed[None], scores, NEGATIVE)
        row_top = jnp.max(masked, axis=2, keepdims=True)
        exponent = jnp.where(allowed[None], jnp.exp(masked - row_top), 0.0)
        denominator = jnp.sum(exponent, axis=2)
        numerator = jnp.einsum(
            "hqk,khd->qhd",
            exponent.astype(jnp.bfloat16),
            value_all,
            preferred_element_type=jnp.float32,
        )
        return (numerator / denominator.T[:, :, None]).astype(jnp.bfloat16)

    block_starts = jnp.arange(block_count, dtype=jnp.int32) * block_len
    heads_out = lax.map(query_block, block_starts).reshape(group_len, head_width)
    head_count = lax.axis_size("head")
    head_terms = jnp.dot(heads_out, out_weight, preferred_element_type=jnp.float32).astype(
        jnp.bfloat16
    )
    head_terms = lax.all_to_all(
        head_terms.reshape(head_count, local_rows, D), "head", split_axis=0, concat_axis=0, tiled=True
    )
    attn_rows = jnp.sum(head_terms.astype(jnp.float32), axis=0)
    stream = (tokens.astype(jnp.float32) + attn_rows).reshape(local_rows // 4, 4, D)
    average = jnp.sum(stream, axis=2, keepdims=True) / D
    variance = jnp.sum(stream * stream, axis=2, keepdims=True) / D - average * average
    window_rows = ((stream - average) * lax.rsqrt(variance + EPSILON) * merge_gain).astype(
        jnp.bfloat16
    )
    merged_slice = lax.all_to_all(
        window_rows.reshape(local_rows // 4, 4 * D), "head", split_axis=1, concat_axis=0, tiled=True
    )
    merged_count = local_rows // 4
    column_terms = jnp.dot(
        merged_slice,
        full_merge_weight,
        preferred_element_type=jnp.float32,
    )
    column_terms = lax.all_to_all(
        column_terms.astype(jnp.bfloat16).reshape(head_count, merged_count, -1),
        "head",
        split_axis=0,
        concat_axis=0,
        tiled=True,
    )
    projected = jnp.sum(column_terms.astype(jnp.float32), axis=0).astype(jnp.bfloat16)
    slot_count = max(2, 2 * merged_count // tok_count)
    owner_col = owners[:, 0]
    owner_hot = (owner_col[:, None] == jnp.arange(tok_count, dtype=jnp.int32)[None, :]).astype(
        jnp.int32
    )
    earlier = jnp.cumsum(owner_hot, axis=0, dtype=jnp.int32) - owner_hot
    slot_index = jnp.sum(earlier * owner_hot, axis=1, dtype=jnp.int32)
    target = owner_col * slot_count + slot_index
    select = (
        jnp.arange(tok_count * slot_count, dtype=jnp.int32)[:, None] == target[None, :]
    ).astype(jnp.bfloat16)
    send_rows = jnp.dot(select, projected, preferred_element_type=jnp.float32).astype(jnp.bfloat16)
    send_rows = send_rows.reshape(tok_count, slot_count, -1)
    received = lax.all_to_all(send_rows, "tok", split_axis=0, concat_axis=0, tiled=True)
    return received.reshape(tok_count * slot_count, -1)


def solution(mesh):
    placed = (
        P(("tok", "head"), None),
        P(),
        P(None, "head", None),
        P("head", None),
        P(),
        P("head", "tok"),
        P(None, "tok"),
        P("tok"),
        P(None, "tok"),
        P("tok"),
        P(("tok", "head"), None),
    )
    return jax.shard_map(
        body, mesh=mesh, in_specs=placed, out_specs=P(("tok", "head"), None), check_vma=False
    )
```

```python
import jax
import jax.numpy as jnp
from jax import lax
from jax.sharding import PartitionSpec as P

D = 1664
HD = 104
SIDE = 16
TOK = ("tx", "tz")
HEAD = ("hy", "hc")
Z_SIZE = 8


EPSILON = 1e-06
NEGATIVE = -1e30


def layer_norm(values, gain_vec):
    average = jnp.mean(values, axis=-1, keepdims=True)
    centred = values - average
    variance = jnp.mean(centred * centred, axis=-1, keepdims=True)
    return centred * lax.rsqrt(variance + EPSILON) * gain_vec


def rotate(vectors, row_coord, col_coord):
    quarter = vectors.shape[-1] // 4
    frequency = 10000.0 ** (-jnp.arange(quarter, dtype=jnp.float32) / quarter)
    pieces = []
    for which_axis, coordinate in ((0, row_coord), (1, col_coord)):
        leading = vectors[..., 2 * which_axis * quarter : (2 * which_axis + 1) * quarter]
        trailing = vectors[..., (2 * which_axis + 1) * quarter : (2 * which_axis + 2) * quarter]
        angles = coordinate[:, None, None] * frequency
        cosine = jnp.cos(angles)
        sine_val = jnp.sin(angles)
        pieces.append(leading * cosine - trailing * sine_val)
        pieces.append(leading * sine_val + trailing * cosine)
    return jnp.concatenate(pieces, axis=-1)


def body(
    tokens,
    attn_gain,
    qkv_weight,
    out_weight,
    merge_gain,
    merge_weight,
    grid_sizes,
    segment_ids,
    patch_pos,
    live_mask,
    owners,
):
    group_len = segment_ids.shape[0]
    local_rows = tokens.shape[0]
    head_width = qkv_weight.shape[1]
    heads_here = head_width // HD
    tok_count = lax.axis_size("tx") * lax.axis_size("tz")
    image_count = grid_sizes.shape[1]
    local_image = segment_ids - (lax.axis_index("tx") * lax.axis_size("tz") + lax.axis_index("tz")) * image_count
    image_match = local_image[:, None] == jnp.arange(image_count, dtype=jnp.int32)[None, :]
    grid_float = grid_sizes.astype(jnp.float32)
    row_size = jnp.sum(jnp.where(image_match, grid_float[0][None, :], 0.0), axis=1)
    col_size = jnp.sum(jnp.where(image_match, grid_float[1][None, :], 0.0), axis=1)
    row_coord = patch_pos[0].astype(jnp.float32) * SIDE / row_size
    col_coord = patch_pos[1].astype(jnp.float32) * SIDE / col_size
    stacked_weight = qkv_weight.reshape(3 * head_width, D)
    full_merge_weight = lax.all_gather(merge_weight, TOK, axis=1, tiled=True)
    projected_rows = lax.dot_general(
        layer_norm(
            lax.all_gather(tokens, HEAD, axis=0, tiled=True).astype(jnp.float32), attn_gain
        ).astype(jnp.bfloat16),
        stacked_weight,
        (((1,), (1,)), ((), ())),
        preferred_element_type=jnp.float32,
    )
    projected_rows = projected_rows.reshape(group_len, 3, heads_here, HD)
    query_all = (rotate(projected_rows[:, 0], row_coord, col_coord) * HD ** (-0.5)).astype(
        jnp.bfloat16
    )
    key_all = rotate(projected_rows[:, 1], row_coord, col_coord).astype(jnp.bfloat16)
    value_all = projected_rows[:, 2].astype(jnp.bfloat16)
    block_len = min(1024, group_len)
    block_count = group_len // block_len
    key_live = live_mask == 1

    def allowed_pairs(query_start, span):
        query_seg = lax.dynamic_slice_in_dim(segment_ids, query_start, block_len)
        query_place = query_start + jnp.arange(block_len, dtype=jnp.int32)
        key_place = jnp.arange(span, dtype=jnp.int32)
        same_image = query_seg[:, None] == segment_ids[None, :]
        return same_image & (key_live[None, :] | (query_place[:, None] == key_place[None, :]))

    def query_block(query_start):
        queries = lax.dynamic_slice_in_dim(query_all, query_start, block_len, 0)
        allowed = allowed_pairs(query_start, group_len)
        scores = jnp.einsum("qhd,khd->hqk", queries, key_all, preferred_element_type=jnp.float32)
        masked = jnp.where(allowed[None], scores, NEGATIVE)
        row_top = jnp.max(masked, axis=2, keepdims=True)
        exponent = jnp.where(allowed[None], jnp.exp(masked - row_top), 0.0)
        denominator = jnp.sum(exponent, axis=2)
        numerator = jnp.einsum(
            "hqk,khd->qhd",
            exponent.astype(jnp.bfloat16),
            value_all,
            preferred_element_type=jnp.float32,
        )
        return (numerator / denominator.T[:, :, None]).astype(jnp.bfloat16)

    block_starts = jnp.arange(block_count, dtype=jnp.int32) * block_len
    heads_out = lax.map(query_block, block_starts).reshape(group_len, head_width)
    head_count = lax.axis_size(HEAD)
    head_terms = jnp.dot(heads_out, out_weight, preferred_element_type=jnp.float32).astype(
        jnp.bfloat16
    )
    head_terms = lax.all_to_all(
        head_terms.reshape(head_count, local_rows, D), HEAD, split_axis=0, concat_axis=0, tiled=True
    )
    attn_rows = jnp.sum(head_terms.astype(jnp.float32), axis=0)
    stream = (tokens.astype(jnp.float32) + attn_rows).reshape(local_rows // 4, 4, D)
    average = jnp.sum(stream, axis=2, keepdims=True) / D
    variance = jnp.sum(stream * stream, axis=2, keepdims=True) / D - average * average
    window_rows = ((stream - average) * lax.rsqrt(variance + EPSILON) * merge_gain).astype(
        jnp.bfloat16
    )
    merged_slice = lax.all_to_all(
        window_rows.reshape(local_rows // 4, 4 * D), HEAD, split_axis=1, concat_axis=0, tiled=True
    )
    merged_count = local_rows // 4
    y_count = lax.axis_size("hy")
    core_count = lax.axis_size("hc")
    by_core = merged_slice.reshape(y_count, core_count, merged_count, -1)
    by_core = jnp.swapaxes(by_core, 0, 1).reshape(head_count * merged_count, -1)
    column_terms = jnp.dot(by_core, full_merge_weight, preferred_element_type=jnp.float32)
    column_terms = lax.all_to_all(
        column_terms.astype(jnp.bfloat16).reshape(core_count, y_count * merged_count, -1),
        "hc",
        split_axis=0,
        concat_axis=0,
        tiled=True,
    )
    chip_terms = jnp.sum(column_terms.astype(jnp.float32), axis=0).astype(jnp.bfloat16)
    chip_terms = lax.all_to_all(
        chip_terms.reshape(y_count, merged_count, -1), "hy", split_axis=0, concat_axis=0, tiled=True
    )
    projected = jnp.sum(chip_terms.astype(jnp.float32), axis=0).astype(jnp.bfloat16)
    slot_count = max(2, 2 * merged_count // tok_count)
    owner_col = owners[:, 0]
    owner_hot = (owner_col[:, None] == jnp.arange(tok_count, dtype=jnp.int32)[None, :]).astype(
        jnp.int32
    )
    earlier = jnp.cumsum(owner_hot, axis=0, dtype=jnp.int32) - owner_hot
    slot_index = jnp.sum(earlier * owner_hot, axis=1, dtype=jnp.int32)
    target = owner_col * slot_count + slot_index
    select = (
        jnp.arange(tok_count * slot_count, dtype=jnp.int32)[:, None] == target[None, :]
    ).astype(jnp.bfloat16)
    send_rows = jnp.dot(select, projected, preferred_element_type=jnp.float32).astype(jnp.bfloat16)
    send_rows = send_rows.reshape(tok_count, slot_count, -1)
    received = lax.all_to_all(send_rows, TOK, split_axis=0, concat_axis=0, tiled=True)
    return received.reshape(tok_count * slot_count, -1)


def solution(mesh):
    tok_size, head_size = (mesh.shape[name] for name in mesh.axis_names)
    split_mesh = jax.sharding.Mesh(
        mesh.devices.reshape(tok_size // Z_SIZE, Z_SIZE, head_size // 2, 2), TOK + HEAD
    )
    placed = (
        P(TOK + HEAD, None),
        P(),
        P(None, HEAD, None),
        P(HEAD, None),
        P(),
        P(HEAD, TOK),
        P(None, TOK),
        P(TOK),
        P(None, TOK),
        P(TOK),
        P(TOK + HEAD, None),
    )
    return jax.shard_map(
        body, mesh=split_mesh, in_specs=placed, out_specs=P(TOK + HEAD, None), check_vma=False
    )
```

```python
import jax
import jax.numpy as jnp
from jax import lax
from jax.sharding import PartitionSpec as P

D = 1664
HD = 104
SIDE = 16
TOK = ("tx", "tz")
HEAD = ("hy", "hc")
Z_SIZE = 8


EPSILON = 1e-06
NEGATIVE = -1e30


def layer_norm(values, gain_vec):
    average = jnp.mean(values, axis=-1, keepdims=True)
    centred = values - average
    variance = jnp.mean(centred * centred, axis=-1, keepdims=True)
    return centred * lax.rsqrt(variance + EPSILON) * gain_vec


def rotate(vectors, row_coord, col_coord):
    quarter = vectors.shape[-1] // 4
    frequency = 10000.0 ** (-jnp.arange(quarter, dtype=jnp.float32) / quarter)
    pieces = []
    for which_axis, coordinate in ((0, row_coord), (1, col_coord)):
        leading = vectors[..., 2 * which_axis * quarter : (2 * which_axis + 1) * quarter]
        trailing = vectors[..., (2 * which_axis + 1) * quarter : (2 * which_axis + 2) * quarter]
        angles = coordinate[:, None, None] * frequency
        cosine = jnp.cos(angles)
        sine_val = jnp.sin(angles)
        pieces.append(leading * cosine - trailing * sine_val)
        pieces.append(leading * sine_val + trailing * cosine)
    return jnp.concatenate(pieces, axis=-1)


def body(
    tokens,
    attn_gain,
    qkv_weight,
    out_weight,
    merge_gain,
    merge_weight,
    grid_sizes,
    segment_ids,
    patch_pos,
    live_mask,
    owners,
):
    group_len = segment_ids.shape[0]
    local_rows = tokens.shape[0]
    head_width = qkv_weight.shape[1]
    heads_here = head_width // HD
    tok_count = lax.axis_size("tx") * lax.axis_size("tz")
    image_count = grid_sizes.shape[1]
    local_image = segment_ids - (lax.axis_index("tx") * lax.axis_size("tz") + lax.axis_index("tz")) * image_count
    image_match = local_image[:, None] == jnp.arange(image_count, dtype=jnp.int32)[None, :]
    grid_float = grid_sizes.astype(jnp.float32)
    row_size = jnp.sum(jnp.where(image_match, grid_float[0][None, :], 0.0), axis=1)
    col_size = jnp.sum(jnp.where(image_match, grid_float[1][None, :], 0.0), axis=1)
    row_coord = patch_pos[0].astype(jnp.float32) * SIDE / row_size
    col_coord = patch_pos[1].astype(jnp.float32) * SIDE / col_size
    stacked_weight = qkv_weight.reshape(3 * head_width, D)
    full_merge_weight = lax.all_gather(merge_weight, TOK, axis=1, tiled=True)
    y_count = lax.axis_size("hy")
    core_count = lax.axis_size("hc")
    by_y = lax.all_to_all(
        jnp.broadcast_to(tokens[None], (y_count,) + tokens.shape), "hy", split_axis=0, concat_axis=0, tiled=True
    )
    by_core = lax.all_to_all(
        jnp.broadcast_to(by_y[None], (core_count,) + by_y.shape), "hc", split_axis=0, concat_axis=0, tiled=True
    )
    gathered_tokens = jnp.swapaxes(by_core, 0, 1).reshape(group_len, D)
    projected_rows = lax.dot_general(
        layer_norm(gathered_tokens.astype(jnp.float32), attn_gain).astype(jnp.bfloat16),
        stacked_weight,
        (((1,), (1,)), ((), ())),
        preferred_element_type=jnp.float32,
    )
    projected_rows = projected_rows.reshape(group_len, 3, heads_here, HD)
    query_all = (rotate(projected_rows[:, 0], row_coord, col_coord) * HD ** (-0.5)).astype(
        jnp.bfloat16
    )
    key_all = rotate(projected_rows[:, 1], row_coord, col_coord).astype(jnp.bfloat16)
    value_all = projected_rows[:, 2].astype(jnp.bfloat16)
    block_len = min(1024, group_len)
    block_count = group_len // block_len
    key_live = live_mask == 1

    def allowed_pairs(query_start, span):
        query_seg = lax.dynamic_slice_in_dim(segment_ids, query_start, block_len)
        query_place = query_start + jnp.arange(block_len, dtype=jnp.int32)
        key_place = jnp.arange(span, dtype=jnp.int32)
        same_image = query_seg[:, None] == segment_ids[None, :]
        return same_image & (key_live[None, :] | (query_place[:, None] == key_place[None, :]))

    def query_block(query_start):
        queries = lax.dynamic_slice_in_dim(query_all, query_start, block_len, 0)
        allowed = allowed_pairs(query_start, group_len)
        scores = jnp.einsum("qhd,khd->hqk", queries, key_all, preferred_element_type=jnp.float32)
        masked = jnp.where(allowed[None], scores, NEGATIVE)
        row_top = jnp.max(masked, axis=2, keepdims=True)
        exponent = jnp.where(allowed[None], jnp.exp(masked - row_top), 0.0)
        denominator = jnp.sum(exponent, axis=2)
        numerator = jnp.einsum(
            "hqk,khd->qhd",
            exponent.astype(jnp.bfloat16),
            value_all,
            preferred_element_type=jnp.float32,
        )
        return (numerator / denominator.T[:, :, None]).astype(jnp.bfloat16)

    block_starts = jnp.arange(block_count, dtype=jnp.int32) * block_len
    heads_out = lax.map(query_block, block_starts).reshape(group_len, head_width)
    head_count = lax.axis_size(HEAD)
    heads_by_core = heads_out.reshape(y_count, core_count, local_rows, head_width)
    heads_by_core = jnp.swapaxes(heads_by_core, 0, 1).reshape(group_len, head_width)
    head_terms = jnp.dot(heads_by_core, out_weight, preferred_element_type=jnp.float32).astype(
        jnp.bfloat16
    )
    head_terms = lax.all_to_all(
        head_terms.reshape(core_count, y_count * local_rows, D), "hc", split_axis=0, concat_axis=0, tiled=True
    )
    chip_rows = jnp.sum(head_terms.astype(jnp.float32), axis=0).astype(jnp.bfloat16)
    chip_rows = lax.all_to_all(
        chip_rows.reshape(y_count, local_rows, D), "hy", split_axis=0, concat_axis=0, tiled=True
    )
    attn_rows = jnp.sum(chip_rows.astype(jnp.float32), axis=0)
    stream = (tokens.astype(jnp.float32) + attn_rows).reshape(local_rows // 4, 4, D)
    average = jnp.sum(stream, axis=2, keepdims=True) / D
    variance = jnp.sum(stream * stream, axis=2, keepdims=True) / D - average * average
    window_rows = ((stream - average) * lax.rsqrt(variance + EPSILON) * merge_gain).astype(
        jnp.bfloat16
    )
    merged_slice = lax.all_to_all(
        window_rows.reshape(local_rows // 4, 4 * D), HEAD, split_axis=1, concat_axis=0, tiled=True
    )
    merged_count = local_rows // 4
    by_core = merged_slice.reshape(y_count, core_count, merged_count, -1)
    by_core = jnp.swapaxes(by_core, 0, 1).reshape(head_count * merged_count, -1)
    column_terms = jnp.dot(by_core, full_merge_weight, preferred_element_type=jnp.float32)
    column_terms = lax.all_to_all(
        column_terms.astype(jnp.bfloat16).reshape(core_count, y_count * merged_count, -1),
        "hc",
        split_axis=0,
        concat_axis=0,
        tiled=True,
    )
    chip_terms = jnp.sum(column_terms.astype(jnp.float32), axis=0).astype(jnp.bfloat16)
    chip_terms = lax.all_to_all(
        chip_terms.reshape(y_count, merged_count, -1), "hy", split_axis=0, concat_axis=0, tiled=True
    )
    projected = jnp.sum(chip_terms.astype(jnp.float32), axis=0).astype(jnp.bfloat16)
    slot_count = max(2, 2 * merged_count // tok_count)
    owner_col = owners[:, 0]
    owner_hot = (owner_col[:, None] == jnp.arange(tok_count, dtype=jnp.int32)[None, :]).astype(
        jnp.int32
    )
    earlier = jnp.cumsum(owner_hot, axis=0, dtype=jnp.int32) - owner_hot
    slot_index = jnp.sum(earlier * owner_hot, axis=1, dtype=jnp.int32)
    target = owner_col * slot_count + slot_index
    select = (
        jnp.arange(tok_count * slot_count, dtype=jnp.int32)[:, None] == target[None, :]
    ).astype(jnp.bfloat16)
    send_rows = jnp.dot(select, projected, preferred_element_type=jnp.float32).astype(jnp.bfloat16)
    send_rows = send_rows.reshape(tok_count, slot_count, -1)
    received = lax.all_to_all(send_rows, TOK, split_axis=0, concat_axis=0, tiled=True)
    return received.reshape(tok_count * slot_count, -1)


def solution(mesh):
    tok_size, head_size = (mesh.shape[name] for name in mesh.axis_names)
    split_mesh = jax.sharding.Mesh(
        mesh.devices.reshape(tok_size // Z_SIZE, Z_SIZE, head_size // 2, 2), TOK + HEAD
    )
    placed = (
        P(TOK + HEAD, None),
        P(),
        P(None, HEAD, None),
        P(HEAD, None),
        P(),
        P(HEAD, TOK),
        P(None, TOK),
        P(TOK),
        P(None, TOK),
        P(TOK),
        P(TOK + HEAD, None),
    )
    return jax.shard_map(body, mesh=split_mesh, in_specs=placed, out_specs=P(TOK + HEAD, None), check_vma=False)
```

```python
import jax
import jax.numpy as jnp
from jax import lax
from jax.sharding import PartitionSpec as P

D = 1664
HD = 104
SIDE = 16
TOK = ("tx", "tz")
HEAD = ("hy", "hc")
Z_SIZE = 8


EPSILON = 1e-06
NEGATIVE = -1e30


def layer_norm(values, gain_vec):
    average = jnp.mean(values, axis=-1, keepdims=True)
    centred = values - average
    variance = jnp.mean(centred * centred, axis=-1, keepdims=True)
    return centred * lax.rsqrt(variance + EPSILON) * gain_vec


def rotate(vectors, row_coord, col_coord):
    quarter = vectors.shape[-1] // 4
    frequency = 10000.0 ** (-jnp.arange(quarter, dtype=jnp.float32) / quarter)
    pieces = []
    for which_axis, coordinate in ((0, row_coord), (1, col_coord)):
        leading = vectors[..., 2 * which_axis * quarter : (2 * which_axis + 1) * quarter]
        trailing = vectors[..., (2 * which_axis + 1) * quarter : (2 * which_axis + 2) * quarter]
        angles = coordinate[:, None, None] * frequency
        cosine = jnp.cos(angles)
        sine_val = jnp.sin(angles)
        pieces.append(leading * cosine - trailing * sine_val)
        pieces.append(leading * sine_val + trailing * cosine)
    return jnp.concatenate(pieces, axis=-1)


def body(
    tokens,
    attn_gain,
    qkv_weight,
    out_weight,
    merge_gain,
    merge_weight,
    grid_sizes,
    segment_ids,
    patch_pos,
    live_mask,
    owners,
):
    group_len = segment_ids.shape[0]
    local_rows = tokens.shape[0]
    head_width = qkv_weight.shape[1]
    heads_here = head_width // HD
    tok_count = lax.axis_size("tx") * lax.axis_size("tz")
    image_count = grid_sizes.shape[1]
    local_image = segment_ids - (lax.axis_index("tx") * lax.axis_size("tz") + lax.axis_index("tz")) * image_count
    image_match = local_image[:, None] == jnp.arange(image_count, dtype=jnp.int32)[None, :]
    grid_float = grid_sizes.astype(jnp.float32)
    row_size = jnp.sum(jnp.where(image_match, grid_float[0][None, :], 0.0), axis=1)
    col_size = jnp.sum(jnp.where(image_match, grid_float[1][None, :], 0.0), axis=1)
    row_coord = patch_pos[0].astype(jnp.float32) * SIDE / row_size
    col_coord = patch_pos[1].astype(jnp.float32) * SIDE / col_size
    stacked_weight = qkv_weight.reshape(3 * head_width, D)
    full_merge_weight = lax.all_gather(merge_weight, TOK, axis=1, tiled=True)
    y_count = lax.axis_size("hy")
    core_count = lax.axis_size("hc")
    by_y = lax.all_to_all(
        jnp.broadcast_to(tokens[None], (y_count,) + tokens.shape), "hy", split_axis=0, concat_axis=0, tiled=True
    )
    by_core = lax.all_to_all(
        jnp.broadcast_to(by_y[None], (core_count,) + by_y.shape), "hc", split_axis=0, concat_axis=0, tiled=True
    )
    gathered_tokens = jnp.swapaxes(by_core, 0, 1).reshape(group_len, D)
    projected_rows = lax.dot_general(
        layer_norm(gathered_tokens.astype(jnp.float32), attn_gain).astype(jnp.bfloat16),
        stacked_weight,
        (((1,), (1,)), ((), ())),
        preferred_element_type=jnp.float32,
    )
    projected_rows = projected_rows.reshape(group_len, 3, heads_here, HD)
    query_all = (rotate(projected_rows[:, 0], row_coord, col_coord) * HD ** (-0.5)).astype(
        jnp.bfloat16
    )
    key_all = rotate(projected_rows[:, 1], row_coord, col_coord).astype(jnp.bfloat16)
    value_all = projected_rows[:, 2].astype(jnp.bfloat16)
    block_len = min(1024, group_len)
    block_count = group_len // block_len
    key_live = live_mask == 1

    def allowed_pairs(query_start, span):
        query_seg = lax.dynamic_slice_in_dim(segment_ids, query_start, block_len)
        query_place = query_start + jnp.arange(block_len, dtype=jnp.int32)
        key_place = jnp.arange(span, dtype=jnp.int32)
        same_image = query_seg[:, None] == segment_ids[None, :]
        return same_image & (key_live[None, :] | (query_place[:, None] == key_place[None, :]))

    def query_block(query_start):
        queries = lax.dynamic_slice_in_dim(query_all, query_start, block_len, 0)
        allowed = allowed_pairs(query_start, group_len)
        scores = jnp.einsum("qhd,khd->hqk", queries, key_all, preferred_element_type=jnp.float32)
        masked = jnp.where(allowed[None], scores, NEGATIVE)
        row_top = jnp.max(masked, axis=2, keepdims=True)
        exponent = jnp.where(allowed[None], jnp.exp(masked - row_top), 0.0)
        denominator = jnp.sum(exponent, axis=2)
        numerator = jnp.einsum(
            "hqk,khd->qhd",
            exponent.astype(jnp.bfloat16),
            value_all,
            preferred_element_type=jnp.float32,
        )
        return (numerator / denominator.T[:, :, None]).astype(jnp.bfloat16)

    block_starts = jnp.arange(block_count, dtype=jnp.int32) * block_len
    heads_out = lax.map(query_block, block_starts).reshape(group_len, head_width)
    head_count = lax.axis_size(HEAD)
    heads_by_core = heads_out.reshape(y_count, core_count, local_rows, head_width)
    heads_by_core = jnp.swapaxes(heads_by_core, 0, 1).reshape(group_len, head_width)
    head_terms = jnp.dot(heads_by_core, out_weight, preferred_element_type=jnp.float32).astype(
        jnp.bfloat16
    )
    head_terms = lax.all_to_all(
        head_terms.reshape(core_count, y_count * local_rows, D), "hc", split_axis=0, concat_axis=0, tiled=True
    )
    chip_rows = jnp.sum(head_terms.astype(jnp.float32), axis=0).astype(jnp.bfloat16)
    chip_rows = lax.all_to_all(
        chip_rows.reshape(y_count, local_rows, D), "hy", split_axis=0, concat_axis=0, tiled=True
    )
    attn_rows = jnp.sum(chip_rows.astype(jnp.float32), axis=0)
    stream = (tokens.astype(jnp.float32) + attn_rows).reshape(local_rows // 4, 4, D)
    average = jnp.sum(stream, axis=2, keepdims=True) / D
    variance = jnp.sum(stream * stream, axis=2, keepdims=True) / D - average * average
    window_rows = ((stream - average) * lax.rsqrt(variance + EPSILON) * merge_gain).astype(
        jnp.bfloat16
    )
    window_rows = window_rows.reshape(local_rows // 4, y_count, core_count, -1)
    window_rows = jnp.transpose(window_rows, (2, 1, 0, 3))
    window_rows = lax.all_to_all(window_rows, "hc", split_axis=0, concat_axis=0, tiled=True)
    window_rows = jnp.swapaxes(window_rows, 0, 1)
    merged_slice = lax.all_to_all(window_rows, "hy", split_axis=0, concat_axis=0, tiled=True)
    merged_slice = merged_slice.reshape(head_count * (local_rows // 4), -1)
    merged_count = local_rows // 4
    by_core = merged_slice.reshape(y_count, core_count, merged_count, -1)
    by_core = jnp.swapaxes(by_core, 0, 1).reshape(head_count * merged_count, -1)
    column_terms = jnp.dot(by_core, full_merge_weight, preferred_element_type=jnp.float32)
    column_terms = lax.all_to_all(
        column_terms.astype(jnp.bfloat16).reshape(core_count, y_count * merged_count, -1),
        "hc",
        split_axis=0,
        concat_axis=0,
        tiled=True,
    )
    chip_terms = jnp.sum(column_terms.astype(jnp.float32), axis=0).astype(jnp.bfloat16)
    chip_terms = lax.all_to_all(
        chip_terms.reshape(y_count, merged_count, -1), "hy", split_axis=0, concat_axis=0, tiled=True
    )
    projected = jnp.sum(chip_terms.astype(jnp.float32), axis=0).astype(jnp.bfloat16)
    slot_count = max(2, 2 * merged_count // tok_count)
    owner_col = owners[:, 0]
    owner_hot = (owner_col[:, None] == jnp.arange(tok_count, dtype=jnp.int32)[None, :]).astype(
        jnp.int32
    )
    earlier = jnp.cumsum(owner_hot, axis=0, dtype=jnp.int32) - owner_hot
    slot_index = jnp.sum(earlier * owner_hot, axis=1, dtype=jnp.int32)
    target = owner_col * slot_count + slot_index
    select = (
        jnp.arange(tok_count * slot_count, dtype=jnp.int32)[:, None] == target[None, :]
    ).astype(jnp.bfloat16)
    send_rows = jnp.dot(select, projected, preferred_element_type=jnp.float32).astype(jnp.bfloat16)
    send_rows = send_rows.reshape(tok_count, slot_count, -1)
    received = lax.all_to_all(send_rows, TOK, split_axis=0, concat_axis=0, tiled=True)
    return received.reshape(tok_count * slot_count, -1)


def solution(mesh):
    tok_size, head_size = (mesh.shape[name] for name in mesh.axis_names)
    split_mesh = jax.sharding.Mesh(
        mesh.devices.reshape(tok_size // Z_SIZE, Z_SIZE, head_size // 2, 2), TOK + HEAD
    )
    placed = (
        P(TOK + HEAD, None),
        P(),
        P(None, HEAD, None),
        P(HEAD, None),
        P(),
        P(HEAD, TOK),
        P(None, TOK),
        P(TOK),
        P(None, TOK),
        P(TOK),
        P(TOK + HEAD, None),
    )
    return jax.shard_map(body, mesh=split_mesh, in_specs=placed, out_specs=P(TOK + HEAD, None), check_vma=False)
```

```python
import jax
import jax.numpy as jnp
from jax import lax
from jax.sharding import PartitionSpec as P

D = 1664
HD = 104
SIDE = 16
TOK = ("tx", "tz")
HEAD = ("hy", "hc")
Z_SIZE = 8


EPSILON = 1e-06
NEGATIVE = -1e30


def layer_norm(values, gain_vec):
    average = jnp.mean(values, axis=-1, keepdims=True)
    centred = values - average
    variance = jnp.mean(centred * centred, axis=-1, keepdims=True)
    return centred * lax.rsqrt(variance + EPSILON) * gain_vec


def rotate(vectors, row_coord, col_coord):
    quarter = vectors.shape[-1] // 4
    frequency = 10000.0 ** (-jnp.arange(quarter, dtype=jnp.float32) / quarter)
    pieces = []
    for which_axis, coordinate in ((0, row_coord), (1, col_coord)):
        leading = vectors[..., 2 * which_axis * quarter : (2 * which_axis + 1) * quarter]
        trailing = vectors[..., (2 * which_axis + 1) * quarter : (2 * which_axis + 2) * quarter]
        angles = coordinate[:, None, None] * frequency
        cosine = jnp.cos(angles)
        sine_val = jnp.sin(angles)
        pieces.append(leading * cosine - trailing * sine_val)
        pieces.append(leading * sine_val + trailing * cosine)
    return jnp.concatenate(pieces, axis=-1)


def body(
    tokens,
    attn_gain,
    qkv_weight,
    out_weight,
    merge_gain,
    merge_weight,
    grid_sizes,
    segment_ids,
    patch_pos,
    live_mask,
    owners,
):
    group_len = segment_ids.shape[0]
    local_rows = tokens.shape[0]
    head_width = qkv_weight.shape[1]
    heads_here = head_width // HD
    tok_count = lax.axis_size("tx") * lax.axis_size("tz")
    image_count = grid_sizes.shape[1]
    local_image = segment_ids - (lax.axis_index("tx") * lax.axis_size("tz") + lax.axis_index("tz")) * image_count
    image_match = local_image[:, None] == jnp.arange(image_count, dtype=jnp.int32)[None, :]
    grid_float = grid_sizes.astype(jnp.float32)
    row_size = jnp.sum(jnp.where(image_match, grid_float[0][None, :], 0.0), axis=1)
    col_size = jnp.sum(jnp.where(image_match, grid_float[1][None, :], 0.0), axis=1)
    row_coord = patch_pos[0].astype(jnp.float32) * SIDE / row_size
    col_coord = patch_pos[1].astype(jnp.float32) * SIDE / col_size
    stacked_weight = qkv_weight.reshape(3 * head_width, D)
    full_merge_weight = lax.all_gather(merge_weight, TOK, axis=1, tiled=True)
    y_count = lax.axis_size("hy")
    core_count = lax.axis_size("hc")
    by_y = lax.all_to_all(
        jnp.broadcast_to(tokens[None], (y_count,) + tokens.shape), "hy", split_axis=0, concat_axis=0, tiled=True
    )
    partner = lax.ppermute(by_y, "hc", [(0, 1), (1, 0)])
    first_core = lax.axis_index("hc") == 0
    pair = jnp.stack(
        [jnp.where(first_core, by_y, partner), jnp.where(first_core, partner, by_y)], axis=1
    )
    gathered_tokens = pair.reshape(group_len, D)
    projected_rows = lax.dot_general(
        layer_norm(gathered_tokens.astype(jnp.float32), attn_gain).astype(jnp.bfloat16),
        stacked_weight,
        (((1,), (1,)), ((), ())),
        preferred_element_type=jnp.float32,
    )
    projected_rows = projected_rows.reshape(group_len, 3, heads_here, HD)
    query_all = (rotate(projected_rows[:, 0], row_coord, col_coord) * HD ** (-0.5)).astype(
        jnp.bfloat16
    )
    key_all = rotate(projected_rows[:, 1], row_coord, col_coord).astype(jnp.bfloat16)
    value_all = projected_rows[:, 2].astype(jnp.bfloat16)
    block_len = min(1024, group_len)
    block_count = group_len // block_len
    key_live = live_mask == 1

    def allowed_pairs(query_start, span):
        query_seg = lax.dynamic_slice_in_dim(segment_ids, query_start, block_len)
        query_place = query_start + jnp.arange(block_len, dtype=jnp.int32)
        key_place = jnp.arange(span, dtype=jnp.int32)
        same_image = query_seg[:, None] == segment_ids[None, :]
        return same_image & (key_live[None, :] | (query_place[:, None] == key_place[None, :]))

    def query_block(query_start):
        queries = lax.dynamic_slice_in_dim(query_all, query_start, block_len, 0)
        allowed = allowed_pairs(query_start, group_len)
        scores = jnp.einsum("qhd,khd->hqk", queries, key_all, preferred_element_type=jnp.float32)
        masked = jnp.where(allowed[None], scores, NEGATIVE)
        row_top = jnp.max(masked, axis=2, keepdims=True)
        exponent = jnp.where(allowed[None], jnp.exp(masked - row_top), 0.0)
        denominator = jnp.sum(exponent, axis=2)
        numerator = jnp.einsum(
            "hqk,khd->qhd",
            exponent.astype(jnp.bfloat16),
            value_all,
            preferred_element_type=jnp.float32,
        )
        return (numerator / denominator.T[:, :, None]).astype(jnp.bfloat16)

    block_starts = jnp.arange(block_count, dtype=jnp.int32) * block_len
    heads_out = lax.map(query_block, block_starts).reshape(group_len, head_width)
    head_count = lax.axis_size(HEAD)
    heads_by_core = heads_out.reshape(y_count, core_count, local_rows, head_width)
    heads_by_core = jnp.swapaxes(heads_by_core, 0, 1).reshape(group_len, head_width)
    head_terms = jnp.dot(heads_by_core, out_weight, preferred_element_type=jnp.float32).astype(
        jnp.bfloat16
    )
    head_terms = lax.all_to_all(
        head_terms.reshape(core_count, y_count * local_rows, D), "hc", split_axis=0, concat_axis=0, tiled=True
    )
    chip_rows = jnp.sum(head_terms.astype(jnp.float32), axis=0).astype(jnp.bfloat16)
    chip_rows = lax.all_to_all(
        chip_rows.reshape(y_count, local_rows, D), "hy", split_axis=0, concat_axis=0, tiled=True
    )
    attn_rows = jnp.sum(chip_rows.astype(jnp.float32), axis=0)
    stream = (tokens.astype(jnp.float32) + attn_rows).reshape(local_rows // 4, 4, D)
    average = jnp.sum(stream, axis=2, keepdims=True) / D
    variance = jnp.sum(stream * stream, axis=2, keepdims=True) / D - average * average
    window_rows = ((stream - average) * lax.rsqrt(variance + EPSILON) * merge_gain).astype(
        jnp.bfloat16
    )
    merged_slice = lax.all_to_all(
        window_rows.reshape(local_rows // 4, 4 * D), HEAD, split_axis=1, concat_axis=0, tiled=True
    )
    merged_count = local_rows // 4
    by_core = merged_slice.reshape(y_count, core_count, merged_count, -1)
    by_core = jnp.swapaxes(by_core, 0, 1).reshape(head_count * merged_count, -1)
    column_terms = jnp.dot(by_core, full_merge_weight, preferred_element_type=jnp.float32)
    column_terms = lax.all_to_all(
        column_terms.astype(jnp.bfloat16).reshape(core_count, y_count * merged_count, -1),
        "hc",
        split_axis=0,
        concat_axis=0,
        tiled=True,
    )
    chip_terms = jnp.sum(column_terms.astype(jnp.float32), axis=0).astype(jnp.bfloat16)
    chip_terms = lax.all_to_all(
        chip_terms.reshape(y_count, merged_count, -1), "hy", split_axis=0, concat_axis=0, tiled=True
    )
    projected = jnp.sum(chip_terms.astype(jnp.float32), axis=0).astype(jnp.bfloat16)
    slot_count = max(2, 2 * merged_count // tok_count)
    owner_col = owners[:, 0]
    owner_hot = (owner_col[:, None] == jnp.arange(tok_count, dtype=jnp.int32)[None, :]).astype(
        jnp.int32
    )
    earlier = jnp.cumsum(owner_hot, axis=0, dtype=jnp.int32) - owner_hot
    slot_index = jnp.sum(earlier * owner_hot, axis=1, dtype=jnp.int32)
    target = owner_col * slot_count + slot_index
    select = (
        jnp.arange(tok_count * slot_count, dtype=jnp.int32)[:, None] == target[None, :]
    ).astype(jnp.bfloat16)
    send_rows = jnp.dot(select, projected, preferred_element_type=jnp.float32).astype(jnp.bfloat16)
    send_rows = send_rows.reshape(tok_count, slot_count, -1)
    received = lax.all_to_all(send_rows, TOK, split_axis=0, concat_axis=0, tiled=True)
    return received.reshape(tok_count * slot_count, -1)


def solution(mesh):
    tok_size, head_size = (mesh.shape[name] for name in mesh.axis_names)
    split_mesh = jax.sharding.Mesh(
        mesh.devices.reshape(tok_size // Z_SIZE, Z_SIZE, head_size // 2, 2), TOK + HEAD
    )
    placed = (
        P(TOK + HEAD, None),
        P(),
        P(None, HEAD, None),
        P(HEAD, None),
        P(),
        P(HEAD, TOK),
        P(None, TOK),
        P(TOK),
        P(None, TOK),
        P(TOK),
        P(TOK + HEAD, None),
    )
    return jax.shard_map(body, mesh=split_mesh, in_specs=placed, out_specs=P(TOK + HEAD, None), check_vma=False)
```

```python
import jax
import jax.numpy as jnp
from jax import lax
from jax.sharding import PartitionSpec as P

D = 1664
HD = 104
SIDE = 16
TOK = ("tx", "tz")
HEAD = ("hy", "hc")
Z_SIZE = 8


EPSILON = 1e-06
NEGATIVE = -1e30


def layer_norm(values, gain_vec):
    average = jnp.mean(values, axis=-1, keepdims=True)
    centred = values - average
    variance = jnp.mean(centred * centred, axis=-1, keepdims=True)
    return centred * lax.rsqrt(variance + EPSILON) * gain_vec


def rotate(vectors, row_coord, col_coord):
    quarter = vectors.shape[-1] // 4
    frequency = 10000.0 ** (-jnp.arange(quarter, dtype=jnp.float32) / quarter)
    pieces = []
    for which_axis, coordinate in ((0, row_coord), (1, col_coord)):
        leading = vectors[..., 2 * which_axis * quarter : (2 * which_axis + 1) * quarter]
        trailing = vectors[..., (2 * which_axis + 1) * quarter : (2 * which_axis + 2) * quarter]
        angles = coordinate[:, None, None] * frequency
        cosine = jnp.cos(angles)
        sine_val = jnp.sin(angles)
        pieces.append(leading * cosine - trailing * sine_val)
        pieces.append(leading * sine_val + trailing * cosine)
    return jnp.concatenate(pieces, axis=-1)


def pair_sum(terms, first_core):
    away = jnp.where(first_core, terms[1], terms[0])
    kept = jnp.where(first_core, terms[0], terms[1])
    arrived = lax.ppermute(away, "hc", [(0, 1), (1, 0)])
    return (kept.astype(jnp.float32) + arrived.astype(jnp.float32)).astype(jnp.bfloat16)


def body(
    tokens,
    attn_gain,
    qkv_weight,
    out_weight,
    merge_gain,
    merge_weight,
    grid_sizes,
    segment_ids,
    patch_pos,
    live_mask,
    owners,
):
    group_len = segment_ids.shape[0]
    local_rows = tokens.shape[0]
    head_width = qkv_weight.shape[1]
    heads_here = head_width // HD
    tok_count = lax.axis_size("tx") * lax.axis_size("tz")
    image_count = grid_sizes.shape[1]
    local_image = segment_ids - (lax.axis_index("tx") * lax.axis_size("tz") + lax.axis_index("tz")) * image_count
    image_match = local_image[:, None] == jnp.arange(image_count, dtype=jnp.int32)[None, :]
    grid_float = grid_sizes.astype(jnp.float32)
    row_size = jnp.sum(jnp.where(image_match, grid_float[0][None, :], 0.0), axis=1)
    col_size = jnp.sum(jnp.where(image_match, grid_float[1][None, :], 0.0), axis=1)
    row_coord = patch_pos[0].astype(jnp.float32) * SIDE / row_size
    col_coord = patch_pos[1].astype(jnp.float32) * SIDE / col_size
    stacked_weight = qkv_weight.reshape(3 * head_width, D)
    full_merge_weight = lax.all_gather(merge_weight, TOK, axis=1, tiled=True)
    y_count = lax.axis_size("hy")
    core_count = lax.axis_size("hc")
    by_y = lax.all_to_all(
        jnp.broadcast_to(tokens[None], (y_count,) + tokens.shape), "hy", split_axis=0, concat_axis=0, tiled=True
    )
    partner = lax.ppermute(by_y, "hc", [(0, 1), (1, 0)])
    first_core = lax.axis_index("hc") == 0
    pair = jnp.stack(
        [jnp.where(first_core, by_y, partner), jnp.where(first_core, partner, by_y)], axis=1
    )
    gathered_tokens = pair.reshape(group_len, D)
    projected_rows = lax.dot_general(
        layer_norm(gathered_tokens.astype(jnp.float32), attn_gain).astype(jnp.bfloat16),
        stacked_weight,
        (((1,), (1,)), ((), ())),
        preferred_element_type=jnp.float32,
    )
    projected_rows = projected_rows.reshape(group_len, 3, heads_here, HD)
    query_all = (rotate(projected_rows[:, 0], row_coord, col_coord) * HD ** (-0.5)).astype(
        jnp.bfloat16
    )
    key_all = rotate(projected_rows[:, 1], row_coord, col_coord).astype(jnp.bfloat16)
    value_all = projected_rows[:, 2].astype(jnp.bfloat16)
    block_len = min(1024, group_len)
    block_count = group_len // block_len
    key_live = live_mask == 1

    def allowed_pairs(query_start, span):
        query_seg = lax.dynamic_slice_in_dim(segment_ids, query_start, block_len)
        query_place = query_start + jnp.arange(block_len, dtype=jnp.int32)
        key_place = jnp.arange(span, dtype=jnp.int32)
        same_image = query_seg[:, None] == segment_ids[None, :]
        return same_image & (key_live[None, :] | (query_place[:, None] == key_place[None, :]))

    def query_block(query_start):
        queries = lax.dynamic_slice_in_dim(query_all, query_start, block_len, 0)
        allowed = allowed_pairs(query_start, group_len)
        scores = jnp.einsum("qhd,khd->hqk", queries, key_all, preferred_element_type=jnp.float32)
        masked = jnp.where(allowed[None], scores, NEGATIVE)
        row_top = jnp.max(masked, axis=2, keepdims=True)
        exponent = jnp.where(allowed[None], jnp.exp(masked - row_top), 0.0)
        denominator = jnp.sum(exponent, axis=2)
        numerator = jnp.einsum(
            "hqk,khd->qhd",
            exponent.astype(jnp.bfloat16),
            value_all,
            preferred_element_type=jnp.float32,
        )
        return (numerator / denominator.T[:, :, None]).astype(jnp.bfloat16)

    block_starts = jnp.arange(block_count, dtype=jnp.int32) * block_len
    heads_out = lax.map(query_block, block_starts).reshape(group_len, head_width)
    head_count = lax.axis_size(HEAD)
    heads_by_core = heads_out.reshape(y_count, core_count, local_rows, head_width)
    heads_by_core = jnp.swapaxes(heads_by_core, 0, 1).reshape(group_len, head_width)
    head_terms = jnp.dot(heads_by_core, out_weight, preferred_element_type=jnp.float32).astype(
        jnp.bfloat16
    )
    head_terms = head_terms.reshape(core_count, y_count * local_rows, D)
    chip_rows = pair_sum(head_terms, first_core)
    chip_rows = lax.all_to_all(
        chip_rows.reshape(y_count, local_rows, D), "hy", split_axis=0, concat_axis=0, tiled=True
    )
    attn_rows = jnp.sum(chip_rows.astype(jnp.float32), axis=0)
    stream = (tokens.astype(jnp.float32) + attn_rows).reshape(local_rows // 4, 4, D)
    average = jnp.sum(stream, axis=2, keepdims=True) / D
    variance = jnp.sum(stream * stream, axis=2, keepdims=True) / D - average * average
    window_rows = ((stream - average) * lax.rsqrt(variance + EPSILON) * merge_gain).astype(
        jnp.bfloat16
    )
    merged_slice = lax.all_to_all(
        window_rows.reshape(local_rows // 4, 4 * D), HEAD, split_axis=1, concat_axis=0, tiled=True
    )
    merged_count = local_rows // 4
    by_core = merged_slice.reshape(y_count, core_count, merged_count, -1)
    by_core = jnp.swapaxes(by_core, 0, 1).reshape(head_count * merged_count, -1)
    column_terms = jnp.dot(by_core, full_merge_weight, preferred_element_type=jnp.float32)
    column_terms = column_terms.astype(jnp.bfloat16).reshape(core_count, y_count * merged_count, -1)
    chip_terms = pair_sum(column_terms, first_core)
    chip_terms = lax.all_to_all(
        chip_terms.reshape(y_count, merged_count, -1), "hy", split_axis=0, concat_axis=0, tiled=True
    )
    projected = jnp.sum(chip_terms.astype(jnp.float32), axis=0).astype(jnp.bfloat16)
    slot_count = max(2, 2 * merged_count // tok_count)
    owner_col = owners[:, 0]
    owner_hot = (owner_col[:, None] == jnp.arange(tok_count, dtype=jnp.int32)[None, :]).astype(
        jnp.int32
    )
    earlier = jnp.cumsum(owner_hot, axis=0, dtype=jnp.int32) - owner_hot
    slot_index = jnp.sum(earlier * owner_hot, axis=1, dtype=jnp.int32)
    target = owner_col * slot_count + slot_index
    select = (
        jnp.arange(tok_count * slot_count, dtype=jnp.int32)[:, None] == target[None, :]
    ).astype(jnp.bfloat16)
    send_rows = jnp.dot(select, projected, preferred_element_type=jnp.float32).astype(jnp.bfloat16)
    send_rows = send_rows.reshape(tok_count, slot_count, -1)
    received = lax.all_to_all(send_rows, TOK, split_axis=0, concat_axis=0, tiled=True)
    return received.reshape(tok_count * slot_count, -1)


def solution(mesh):
    tok_size, head_size = (mesh.shape[name] for name in mesh.axis_names)
    split_mesh = jax.sharding.Mesh(
        mesh.devices.reshape(tok_size // Z_SIZE, Z_SIZE, head_size // 2, 2), TOK + HEAD
    )
    placed = (
        P(TOK + HEAD, None),
        P(),
        P(None, HEAD, None),
        P(HEAD, None),
        P(),
        P(HEAD, TOK),
        P(None, TOK),
        P(TOK),
        P(None, TOK),
        P(TOK),
        P(TOK + HEAD, None),
    )
    return jax.shard_map(
        body, mesh=split_mesh, in_specs=placed, out_specs=P(TOK + HEAD, None), check_vma=False
    )
```

```python
import jax
import jax.numpy as jnp
from jax import lax
from jax.sharding import PartitionSpec as P

D = 1664
HD = 104
SIDE = 16
TOK = ("tx", "tz")
HEAD = ("hy", "hc")
Z_SIZE = 8


EPSILON = 1e-06
NEGATIVE = -1e30


def layer_norm(values, gain_vec):
    average = jnp.mean(values, axis=-1, keepdims=True)
    centred = values - average
    variance = jnp.mean(centred * centred, axis=-1, keepdims=True)
    return centred * lax.rsqrt(variance + EPSILON) * gain_vec


def rotate(vectors, row_coord, col_coord):
    quarter = vectors.shape[-1] // 4
    frequency = 10000.0 ** (-jnp.arange(quarter, dtype=jnp.float32) / quarter)
    pieces = []
    for which_axis, coordinate in ((0, row_coord), (1, col_coord)):
        leading = vectors[..., 2 * which_axis * quarter : (2 * which_axis + 1) * quarter]
        trailing = vectors[..., (2 * which_axis + 1) * quarter : (2 * which_axis + 2) * quarter]
        angles = coordinate[:, None, None] * frequency
        cosine = jnp.cos(angles)
        sine_val = jnp.sin(angles)
        pieces.append(leading * cosine - trailing * sine_val)
        pieces.append(leading * sine_val + trailing * cosine)
    return jnp.concatenate(pieces, axis=-1)


def pair_sum(terms, first_core):
    away = jnp.where(first_core, terms[1], terms[0])
    kept = jnp.where(first_core, terms[0], terms[1])
    arrived = lax.ppermute(away, "hc", [(0, 1), (1, 0)])
    return (kept.astype(jnp.float32) + arrived.astype(jnp.float32)).astype(jnp.bfloat16)


def body(
    tokens,
    attn_gain,
    qkv_weight,
    out_weight,
    merge_gain,
    merge_weight,
    grid_sizes,
    segment_ids,
    patch_pos,
    live_mask,
    owners,
):
    group_len = segment_ids.shape[0]
    local_rows = tokens.shape[0]
    head_width = qkv_weight.shape[1]
    heads_here = head_width // HD
    tok_count = lax.axis_size("tx") * lax.axis_size("tz")
    image_count = grid_sizes.shape[1]
    local_image = segment_ids - (lax.axis_index("tx") * lax.axis_size("tz") + lax.axis_index("tz")) * image_count
    image_match = local_image[:, None] == jnp.arange(image_count, dtype=jnp.int32)[None, :]
    grid_float = grid_sizes.astype(jnp.float32)
    row_size = jnp.sum(jnp.where(image_match, grid_float[0][None, :], 0.0), axis=1)
    col_size = jnp.sum(jnp.where(image_match, grid_float[1][None, :], 0.0), axis=1)
    row_coord = patch_pos[0].astype(jnp.float32) * SIDE / row_size
    col_coord = patch_pos[1].astype(jnp.float32) * SIDE / col_size
    stacked_weight = qkv_weight.reshape(3 * head_width, D)
    full_merge_weight = lax.all_gather(merge_weight, TOK, axis=1, tiled=True)
    y_count = lax.axis_size("hy")
    core_count = lax.axis_size("hc")
    by_y = lax.all_to_all(
        jnp.broadcast_to(tokens[None], (y_count,) + tokens.shape), "hy", split_axis=0, concat_axis=0, tiled=True
    )
    partner = lax.ppermute(by_y, "hc", [(0, 1), (1, 0)])
    first_core = lax.axis_index("hc") == 0
    pair = jnp.stack(
        [jnp.where(first_core, by_y, partner), jnp.where(first_core, partner, by_y)], axis=1
    )
    gathered_tokens = pair.reshape(group_len, D)
    projected_rows = lax.dot_general(
        layer_norm(gathered_tokens.astype(jnp.float32), attn_gain).astype(jnp.bfloat16),
        stacked_weight,
        (((1,), (1,)), ((), ())),
        preferred_element_type=jnp.float32,
    )
    projected_rows = projected_rows.reshape(group_len, 3, heads_here, HD)
    query_all = (rotate(projected_rows[:, 0], row_coord, col_coord) * HD ** (-0.5)).astype(
        jnp.bfloat16
    )
    key_all = rotate(projected_rows[:, 1], row_coord, col_coord).astype(jnp.bfloat16)
    value_all = projected_rows[:, 2].astype(jnp.bfloat16)
    block_len = min(1024, group_len)
    block_count = group_len // block_len
    key_live = live_mask == 1

    def allowed_pairs(query_start, span):
        query_seg = lax.dynamic_slice_in_dim(segment_ids, query_start, block_len)
        query_place = query_start + jnp.arange(block_len, dtype=jnp.int32)
        key_place = jnp.arange(span, dtype=jnp.int32)
        same_image = query_seg[:, None] == segment_ids[None, :]
        return same_image & (key_live[None, :] | (query_place[:, None] == key_place[None, :]))

    def query_block(query_start):
        queries = lax.dynamic_slice_in_dim(query_all, query_start, block_len, 0)
        allowed = allowed_pairs(query_start, group_len)
        scores = jnp.einsum("qhd,khd->hqk", queries, key_all, preferred_element_type=jnp.float32)
        masked = jnp.where(allowed[None], scores, NEGATIVE)
        row_top = jnp.max(masked, axis=2, keepdims=True)
        exponent = jnp.where(allowed[None], jnp.exp(masked - row_top), 0.0)
        denominator = jnp.sum(exponent, axis=2)
        numerator = jnp.einsum(
            "hqk,khd->qhd",
            exponent.astype(jnp.bfloat16),
            value_all,
            preferred_element_type=jnp.float32,
        )
        return (numerator / denominator.T[:, :, None]).astype(jnp.bfloat16)

    block_starts = jnp.arange(block_count, dtype=jnp.int32) * block_len
    heads_out = lax.map(query_block, block_starts).reshape(group_len, head_width)
    head_count = lax.axis_size(HEAD)
    heads_by_core = heads_out.reshape(y_count, core_count, local_rows, head_width)
    heads_by_core = jnp.swapaxes(heads_by_core, 0, 1).reshape(group_len, head_width)
    head_terms = jnp.dot(heads_by_core, out_weight, preferred_element_type=jnp.float32).astype(
        jnp.bfloat16
    )
    head_terms = head_terms.reshape(core_count, y_count * local_rows, D)
    chip_rows = pair_sum(head_terms, first_core)
    chip_rows = lax.all_to_all(
        chip_rows.reshape(y_count, local_rows, D), "hy", split_axis=0, concat_axis=0, tiled=True
    )
    attn_rows = jnp.sum(chip_rows.astype(jnp.float32), axis=0)
    stream = (tokens.astype(jnp.float32) + attn_rows).reshape(local_rows // 4, 4, D)
    average = jnp.sum(stream, axis=2, keepdims=True) / D
    variance = jnp.sum(stream * stream, axis=2, keepdims=True) / D - average * average
    window_rows = ((stream - average) * lax.rsqrt(variance + EPSILON) * merge_gain).astype(
        jnp.bfloat16
    )
    window_rows = window_rows.reshape(local_rows // 4, y_count, core_count, -1)
    window_rows = jnp.transpose(window_rows, (2, 1, 0, 3))
    kept_rows = jnp.where(first_core, window_rows[0], window_rows[1])
    arrived_rows = lax.ppermute(
        jnp.where(first_core, window_rows[1], window_rows[0]), "hc", [(0, 1), (1, 0)]
    )
    core_rows = jnp.stack(
        [jnp.where(first_core, kept_rows, arrived_rows), jnp.where(first_core, arrived_rows, kept_rows)],
        axis=1,
    )
    merged_slice = lax.all_to_all(core_rows, "hy", split_axis=0, concat_axis=0, tiled=True)
    merged_slice = merged_slice.reshape(head_count * (local_rows // 4), -1)
    merged_count = local_rows // 4
    by_core = merged_slice.reshape(y_count, core_count, merged_count, -1)
    by_core = jnp.swapaxes(by_core, 0, 1).reshape(head_count * merged_count, -1)
    column_terms = jnp.dot(by_core, full_merge_weight, preferred_element_type=jnp.float32)
    column_terms = column_terms.astype(jnp.bfloat16).reshape(core_count, y_count * merged_count, -1)
    chip_terms = pair_sum(column_terms, first_core)
    chip_terms = lax.all_to_all(
        chip_terms.reshape(y_count, merged_count, -1), "hy", split_axis=0, concat_axis=0, tiled=True
    )
    projected = jnp.sum(chip_terms.astype(jnp.float32), axis=0).astype(jnp.bfloat16)
    slot_count = max(2, 2 * merged_count // tok_count)
    owner_col = owners[:, 0]
    owner_hot = (owner_col[:, None] == jnp.arange(tok_count, dtype=jnp.int32)[None, :]).astype(
        jnp.int32
    )
    earlier = jnp.cumsum(owner_hot, axis=0, dtype=jnp.int32) - owner_hot
    slot_index = jnp.sum(earlier * owner_hot, axis=1, dtype=jnp.int32)
    target = owner_col * slot_count + slot_index
    select = (
        jnp.arange(tok_count * slot_count, dtype=jnp.int32)[:, None] == target[None, :]
    ).astype(jnp.bfloat16)
    send_rows = jnp.dot(select, projected, preferred_element_type=jnp.float32).astype(jnp.bfloat16)
    send_rows = send_rows.reshape(tok_count, slot_count, -1)
    received = lax.all_to_all(send_rows, TOK, split_axis=0, concat_axis=0, tiled=True)
    return received.reshape(tok_count * slot_count, -1)


def solution(mesh):
    tok_size, head_size = (mesh.shape[name] for name in mesh.axis_names)
    split_mesh = jax.sharding.Mesh(
        mesh.devices.reshape(tok_size // Z_SIZE, Z_SIZE, head_size // 2, 2), TOK + HEAD
    )
    placed = (
        P(TOK + HEAD, None),
        P(),
        P(None, HEAD, None),
        P(HEAD, None),
        P(),
        P(HEAD, TOK),
        P(None, TOK),
        P(TOK),
        P(None, TOK),
        P(TOK),
        P(TOK + HEAD, None),
    )
    return jax.shard_map(body, mesh=split_mesh, in_specs=placed, out_specs=P(TOK + HEAD, None), check_vma=False)
```
